128 devices in a mesh: child: 2 (over z_hi), row: 8 (over y, core), col: 8 (over x, z_lo).
Axes of the slice: x: 4, y: 4, z: 4 (z_hi: 2, z_lo: 2; z = z_hi * 2 + z_lo), core: 2. Of those that a mesh axis runs over, the one named last changes fastest.
Arguments:
- child_fronts: float32 [2, 8192, 8192], P('child', 'row', 'col')
- parent_front: float32 [12288, 12288], P('row', ('child', 'col')), may hold values from -6 to 6
- index_maps: int32 [2, 8192], replicated, may hold values from 0 to 12287, as said below
- orders: int32 [2], replicated, may hold values from 4096 to 8192, as said below
Outputs:
- assembled: float32 [12288, 12288], P('row', ('child', 'col'))
- panel_factor: float32 [2, 8192, 512], P('child', 'row')
The draws below stay inside these ranges and needn't reach their ends.
Inputs may be any that keep to these rules, and one draw needn't show every extreme that they name: For each child, index_maps is one to one. Cut the child indices into aligned blocks of 8192 / 8 and the parent indices into 2 * 8 aligned slices of 12288 / (2 * 8): each block sends exactly 8192 / (2 * 8 * 8) of its indices into each slice. `orders`: one child's order is 8192.
All inputs are finite; a program needn't handle non-finite values.
Results may differ from the reference program's by a relative error of at most 0.0001.
Values sent between devices are 32-bit elements; how exact they have to be, the bound alone decides.
No kernel may reach another device: no remote copies, remote signals or barrier semaphores. Data moves between devices by JAX's collectives and lax.ppermute only.
A program may use at most 128 MiB of HBM per device.

```python
import jax
import jax.numpy as jnp
from jax import lax

PANEL = 512
FRONT = 8192
PARENT = 12288
N_COL = 8


def draw_child_fronts(key, part):
    position = jnp.arange(FRONT)
    noise = jax.random.normal(key, (2, FRONT, FRONT), jnp.float32)
    symmetric = (noise + jnp.swapaxes(noise, 1, 2)) * 0.70710677
    inner = position < PANEL
    both_inner = inner[:, None] & inner[None, :]
    either_inner = inner[:, None] | inner[None, :]
    scaling = jnp.where(both_inner, 0.011, jnp.where(either_inner, 0.12, 1.0)).astype(jnp.float32)
    identity = jnp.where(both_inner & (position[:, None] == position[None, :]), 1.0, 0.0).astype(jnp.float32)
    return symmetric * scaling[None] + identity[None]


def one_map(key):
    block_len = FRONT // N_COL
    slices = 2 * N_COL
    per_block = block_len // slices
    slice_len = PARENT // slices
    per_slice = FRONT // slices
    block_keys = jax.random.split(jax.random.fold_in(key, 5), N_COL)
    block_perms = jax.vmap(lambda k: jax.random.permutation(k, block_len))(block_keys)
    slice_keys = jax.random.split(jax.random.fold_in(key, 9), slices)

    def slots_for(k):
        drawn = jax.random.permutation(k, slice_len)
        return (drawn[:per_slice] + (slice_len - 1 - drawn[0])) % slice_len
    slot_table = jax.vmap(slots_for)(slice_keys)
    block_ids = jnp.arange(N_COL)[:, None]
    slot_ids = jnp.arange(block_len)[None, :]
    slice_ids = slot_ids // per_block
    ranks = block_ids * per_block + (slot_ids - slice_ids * per_block)
    values = slice_ids * slice_len + slot_table[slice_ids, ranks]
    targets = block_ids * block_len + block_perms
    mapping = jnp.zeros((FRONT,), jnp.int32)
    return mapping.at[targets.reshape(-1)].set(values.reshape(-1).astype(jnp.int32))


def draw_index_maps(key, part):
    return jnp.stack([one_map(jax.random.fold_in(key, 31)), one_map(jax.random.fold_in(key, 47))])


def draw_orders(key, part):
    bigger = jax.random.randint(jax.random.fold_in(key, 3), (), 0, 2)
    smaller = FRONT // 2 + jax.random.randint(jax.random.fold_in(key, 4), (), 0, FRONT // 2)
    return jnp.where(jnp.arange(2) == bigger, FRONT, smaller).astype(jnp.int32)


def level_of(key, extent, pieces, smallest, top_value):
    factor_of, own = 1.0, jax.random.fold_in(key, 6)
    for dim, parts in pieces:
        draws = jnp.exp(jax.random.uniform(jax.random.fold_in(own, dim), (parts,), jnp.float32, smallest / len(pieces), top_value / len(pieces)))
        factor_of = factor_of * jnp.repeat(draws, extent[dim] // parts).reshape([-1 if axis == dim else 1 for axis in range(len(extent))])
    return factor_of


def centred(rng, shape, spread, most, shards=(), held_as=jnp.bfloat16):
    values = spread * jax.random.normal(rng, shape, jnp.float32)
    if shards:
        values = values * level_of(rng, shape, shards, -0.22, 0.18)
    return jnp.clip(values, -most, most).astype(held_as)


def setup_inputs(seed: int = 0) -> dict:
    key_list = jax.random.split(jax.random.key(seed), 5)
    return {
        "child_fronts": draw_child_fronts(jax.random.fold_in(key_list[4], 71), 0),
        "parent_front": centred(key_list[1], (PARENT, PARENT), 1.0, 6.0, ((0, 8), (1, 16)), jnp.float32),
        "index_maps": draw_index_maps(jax.random.fold_in(key_list[4], 71), 0),
        "orders": draw_orders(jax.random.fold_in(key_list[4], 71), 0),
    }


def reference(child_fronts, parent_front, index_maps, orders):
    assembled = parent_front
    panels = []
    position = jnp.arange(FRONT, dtype=jnp.int32)
    for source in range(2):
        front_here = child_fronts[source]
        order_here = orders[source]
        diag_factor = jnp.linalg.cholesky(front_here[:PANEL, :PANEL])
        solved = lax.linalg.triangular_solve(diag_factor, front_here[:, :PANEL], left_side=False, lower=True, transpose_a=True)
        top_rows = jnp.pad(diag_factor, ((0, FRONT - PANEL), (0, 0)))
        panel_here = jnp.where(position[:, None] < PANEL, top_rows, solved)
        panel_here = jnp.where(position[:, None] < order_here, panel_here, jnp.float32(0.0))
        panels.append(panel_here)
        update = front_here - jnp.dot(panel_here, panel_here.T, precision=lax.Precision.HIGHEST)
        valid = (position >= PANEL) & (position < order_here)
        update = jnp.where(valid[:, None] & valid[None, :], update, jnp.float32(0.0))
        parent_map = index_maps[source]
        assembled = assembled.at[parent_map[:, None], parent_map[None, :]].add(update)
    return (assembled, jnp.stack(panels))
```

```python
import jax
import jax.numpy as jnp
from jax import lax
from jax.sharding import PartitionSpec as P

PANEL = 512
FRONT = 8192


def from_root(value, axis, source):
    kept = jnp.where(lax.axis_index(axis) == source, value, 0).astype(value.dtype)
    return lax.psum(kept, axis)


def select_rows(parent_map, owner, width, count):
    everywhere = jnp.arange(FRONT, dtype=jnp.int32)
    keyed = jnp.where(parent_map // width == owner, everywhere, everywhere + FRONT)
    chosen = jnp.argsort(keyed)[:count]
    return parent_map[chosen] - owner * width


def invert_slots(slots, length):
    count = slots.shape[0]
    lookup = jnp.full((length,), count, jnp.int32)
    return lookup.at[slots].set(jnp.arange(count, dtype=jnp.int32))


def factor_panel(corner, columns, global_rows, own_order):
    diag_factor = jnp.linalg.cholesky(corner)
    solved = lax.linalg.triangular_solve(
        diag_factor, columns, left_side=False, lower=True, transpose_a=True
    )
    top_rows = jnp.pad(diag_factor, ((0, columns.shape[0] - PANEL), (0, 0)))
    result = jnp.where(global_rows[:, None] < PANEL, top_rows, solved)
    return jnp.where(global_rows[:, None] < own_order, result, jnp.float32(0.0))


def on_device(child_fronts, parent_front, index_maps, orders):
    block_here = child_fronts[0]
    rows_here, cols_here = block_here.shape
    child_index = lax.axis_index("child")
    row_index = lax.axis_index("row")
    col_index = lax.axis_index("col")
    n_row = lax.axis_size("row")
    n_col = lax.axis_size("col")
    own_map = lax.dynamic_index_in_dim(index_maps, child_index, 0, keepdims=False)
    own_order = lax.dynamic_index_in_dim(orders, child_index, 0, keepdims=False)
    global_rows = row_index * rows_here + jnp.arange(rows_here, dtype=jnp.int32)
    global_cols = col_index * cols_here + jnp.arange(cols_here, dtype=jnp.int32)
    columns = from_root(block_here[:, :PANEL], "col", 0)
    corner = from_root(columns[:PANEL], "row", 0)
    own_panel = factor_panel(corner, columns, global_rows, own_order)
    other_panel = from_root(own_panel, "row", col_index)
    update = block_here - jnp.dot(own_panel, other_panel.T, precision=lax.Precision.HIGHEST)
    live_rows = (global_rows >= PANEL) & (global_rows < own_order)
    live_cols = (global_cols >= PANEL) & (global_cols < own_order)
    update = jnp.where(live_rows[:, None] & live_cols[None, :], update, jnp.float32(0.0))
    parent_rows, parent_cols = parent_front.shape
    row_map = lax.dynamic_slice_in_dim(own_map, row_index * rows_here, rows_here)
    col_map = lax.dynamic_slice_in_dim(own_map, col_index * cols_here, cols_here)
    row_keys = row_map // parent_rows * rows_here + jnp.arange(rows_here, dtype=jnp.int32)
    col_keys = col_map // parent_cols * cols_here + jnp.arange(cols_here, dtype=jnp.int32)
    sorted_block = update[jnp.argsort(row_keys)][:, jnp.argsort(col_keys)]
    part_rows = rows_here // n_row
    part_cols = cols_here // (2 * n_col)
    pieces = (
        sorted_block.reshape(n_row, part_rows, 2, n_col, part_cols)
        .transpose(2, 0, 3, 1, 4)
        .reshape(-1, part_cols)
    )
    arrived = lax.all_to_all(
        pieces, ("child", "row", "col"), split_axis=0, concat_axis=0, tiled=True
    )
    arrived = (
        arrived.reshape(2, n_row, n_col, part_rows, part_cols)
        .transpose(0, 1, 3, 2, 4)
        .reshape(2, rows_here, n_col * part_cols)
    )
    col_owner = child_index * n_col + col_index
    assembled = parent_front
    for source in range(2):
        parent_map = index_maps[source]
        row_slots = select_rows(parent_map, row_index, parent_rows, rows_here)
        col_slots = select_rows(parent_map, col_owner, parent_cols, n_col * part_cols)
        row_lookup = invert_slots(row_slots, parent_rows)
        col_lookup = invert_slots(col_slots, parent_cols)
        padded = jnp.pad(arrived[source], ((0, 1), (0, 1)))
        placed = jnp.take(jnp.take(padded, row_lookup, axis=0), col_lookup, axis=1)
        assembled = assembled + placed
    return (assembled, own_panel[None])


def solution(mesh):
    in_specs = (P("child", "row", "col"), P("row", ("child", "col")), P(), P())
    out_specs = (P("row", ("child", "col")), P("child", "row", None))
    return jax.shard_map(
        on_device, mesh=mesh, in_specs=in_specs, out_specs=out_specs, check_vma=False
    )
```

```python
import jax
import jax.numpy as jnp
from jax import lax
from jax.sharding import PartitionSpec as P

PANEL = 512
FRONT = 8192


def from_root(value, axis, source):
    kept = jnp.where(lax.axis_index(axis) == source, value, 0).astype(value.dtype)
    return lax.psum(kept, axis)


def select_rows(parent_map, owner, width, count):
    everywhere = jnp.arange(FRONT, dtype=jnp.int32)
    keyed = jnp.where(parent_map // width == owner, everywhere, everywhere + FRONT)
    chosen = jnp.argsort(keyed)[:count]
    return parent_map[chosen] - owner * width


def invert_slots(slots, length):
    count = slots.shape[0]
    lookup = jnp.full((length,), count, jnp.int32)
    return lookup.at[slots].set(jnp.arange(count, dtype=jnp.int32))


def factor_panel(diag_factor, inverse, columns, global_rows, own_order):
    solved = jnp.dot(columns, inverse.T, precision=lax.Precision.HIGHEST)
    top_rows = jnp.pad(diag_factor, ((0, columns.shape[0] - PANEL), (0, 0)))
    result = jnp.where(global_rows[:, None] < PANEL, top_rows, solved)
    return jnp.where(global_rows[:, None] < own_order, result, jnp.float32(0.0))


def on_device(child_fronts, parent_front, index_maps, orders):
    block_here = child_fronts[0]
    rows_here, cols_here = block_here.shape
    child_index = lax.axis_index("child")
    row_index = lax.axis_index("row")
    col_index = lax.axis_index("col")
    n_row = lax.axis_size("row")
    n_col = lax.axis_size("col")
    own_map = lax.dynamic_index_in_dim(index_maps, child_index, 0, keepdims=False)
    own_order = lax.dynamic_index_in_dim(orders, child_index, 0, keepdims=False)
    global_rows = row_index * rows_here + jnp.arange(rows_here, dtype=jnp.int32)
    global_cols = col_index * cols_here + jnp.arange(cols_here, dtype=jnp.int32)
    columns = from_root(block_here[:, :PANEL], "col", 0)
    sent = jnp.concatenate(
        [
            jnp.where(row_index == col_index, columns, 0),
            jnp.where(row_index == 0, columns[:PANEL], 0),
        ]
    )
    received = lax.psum(sent, "row")
    other_columns, corner = received[:rows_here], received[rows_here:]
    diag_factor = jnp.linalg.cholesky(corner)
    inverse = lax.linalg.triangular_solve(
        diag_factor, jnp.eye(PANEL, dtype=jnp.float32), left_side=True, lower=True
    )
    own_panel = factor_panel(diag_factor, inverse, columns, global_rows, own_order)
    other_panel = factor_panel(diag_factor, inverse, other_columns, global_cols, own_order)
    update = block_here - jnp.dot(own_panel, other_panel.T, precision=lax.Precision.HIGHEST)
    live_rows = (global_rows >= PANEL) & (global_rows < own_order)
    live_cols = (global_cols >= PANEL) & (global_cols < own_order)
    update = jnp.where(live_rows[:, None] & live_cols[None, :], update, jnp.float32(0.0))
    parent_rows, parent_cols = parent_front.shape
    row_map = lax.dynamic_slice_in_dim(own_map, row_index * rows_here, rows_here)
    col_map = lax.dynamic_slice_in_dim(own_map, col_index * cols_here, cols_here)
    row_keys = row_map // parent_rows * rows_here + jnp.arange(rows_here, dtype=jnp.int32)
    col_keys = col_map // parent_cols * cols_here + jnp.arange(cols_here, dtype=jnp.int32)
    sorted_block = update[jnp.argsort(row_keys)][:, jnp.argsort(col_keys)]
    part_rows = rows_here // n_row
    part_cols = cols_here // (2 * n_col)
    pieces = (
        sorted_block.reshape(n_row, part_rows, 2, n_col, part_cols)
        .transpose(2, 0, 3, 1, 4)
        .reshape(-1, part_cols)
    )
    arrived = lax.all_to_all(
        pieces, ("child", "row", "col"), split_axis=0, concat_axis=0, tiled=True
    )
    arrived = (
        arrived.reshape(2, n_row, n_col, part_rows, part_cols)
        .transpose(0, 1, 3, 2, 4)
        .reshape(2, rows_here, n_col * part_cols)
    )
    col_owner = child_index * n_col + col_index
    assembled = parent_front
    for source in range(2):
        parent_map = index_maps[source]
        row_slots = select_rows(parent_map, row_index, parent_rows, rows_here)
        col_slots = select_rows(parent_map, col_owner, parent_cols, n_col * part_cols)
        row_lookup = invert_slots(row_slots, parent_rows)
        col_lookup = invert_slots(col_slots, parent_cols)
        padded = jnp.pad(arrived[source], ((0, 1), (0, 1)))
        placed = jnp.take(jnp.take(padded, row_lookup, axis=0), col_lookup, axis=1)
        assembled = assembled + placed
    return (assembled, own_panel[None])


def solution(mesh):
    in_specs = (P("child", "row", "col"), P("row", ("child", "col")), P(), P())
    out_specs = (P("row", ("child", "col")), P("child", "row", None))
    return jax.shard_map(
        on_device, mesh=mesh, in_specs=in_specs, out_specs=out_specs, check_vma=False
    )
```

```python
import jax
import jax.numpy as jnp
from jax import lax
from jax.sharding import PartitionSpec as P

PANEL = 512
FRONT = 8192


def from_root(value, axis, source):
    kept = jnp.where(lax.axis_index(axis) == source, value, 0).astype(value.dtype)
    return lax.psum(kept, axis)


def spread_sum(value, axis):
    count = lax.axis_size(axis)
    pieces = value.reshape(count, value.shape[0] // count, value.shape[1])
    arrived = lax.all_to_all(pieces, axis, 0, 0, tiled=True)
    return lax.all_gather(arrived.sum(0), axis, axis=0, tiled=True)


def from_first(value, axis):
    count = lax.axis_size(axis)
    pieces = value.reshape(count, value.shape[0] // count, value.shape[1])
    arrived = lax.all_to_all(pieces, axis, 0, 0, tiled=True)
    return lax.all_gather(arrived[0], axis, axis=0, tiled=True)


def select_rows(parent_map, owner, width, count):
    everywhere = jnp.arange(FRONT, dtype=jnp.int32)
    keyed = jnp.where(parent_map // width == owner, everywhere, everywhere + FRONT)
    chosen = jnp.argsort(keyed)[:count]
    return parent_map[chosen] - owner * width


def invert_slots(slots, length):
    count = slots.shape[0]
    lookup = jnp.full((length,), count, jnp.int32)
    return lookup.at[slots].set(jnp.arange(count, dtype=jnp.int32))


def factor_panel(diag_factor, inverse, columns, global_rows, own_order):
    solved = jnp.dot(columns, inverse.T, precision=lax.Precision.HIGHEST)
    top_rows = jnp.pad(diag_factor, ((0, columns.shape[0] - PANEL), (0, 0)))
    result = jnp.where(global_rows[:, None] < PANEL, top_rows, solved)
    return jnp.where(global_rows[:, None] < own_order, result, jnp.float32(0.0))


def on_device(child_fronts, parent_front, index_maps, orders):
    block_here = child_fronts[0]
    rows_here, cols_here = block_here.shape
    child_index = lax.axis_index("child")
    row_index = lax.axis_index("row")
    col_index = lax.axis_index("col")
    n_row = lax.axis_size("row")
    n_col = lax.axis_size("col")
    own_map = lax.dynamic_index_in_dim(index_maps, child_index, 0, keepdims=False)
    own_order = lax.dynamic_index_in_dim(orders, child_index, 0, keepdims=False)
    global_rows = row_index * rows_here + jnp.arange(rows_here, dtype=jnp.int32)
    global_cols = col_index * cols_here + jnp.arange(cols_here, dtype=jnp.int32)
    columns = from_first(block_here[:, :PANEL], "col")
    sent = jnp.concatenate(
        [
            jnp.where(row_index == col_index, columns, 0),
            jnp.where(row_index == 0, columns[:PANEL], 0),
        ]
    )
    received = spread_sum(sent, "row")
    other_columns, corner = received[:rows_here], received[rows_here:]
    diag_factor = jnp.linalg.cholesky(corner)
    inverse = lax.linalg.triangular_solve(
        diag_factor, jnp.eye(PANEL, dtype=jnp.float32), left_side=True, lower=True
    )
    own_panel = factor_panel(diag_factor, inverse, columns, global_rows, own_order)
    other_panel = factor_panel(diag_factor, inverse, other_columns, global_cols, own_order)
    update = block_here - jnp.dot(own_panel, other_panel.T, precision=lax.Precision.HIGHEST)
    live_rows = (global_rows >= PANEL) & (global_rows < own_order)
    live_cols = (global_cols >= PANEL) & (global_cols < own_order)
    update = jnp.where(live_rows[:, None] & live_cols[None, :], update, jnp.float32(0.0))
    parent_rows, parent_cols = parent_front.shape
    row_map = lax.dynamic_slice_in_dim(own_map, row_index * rows_here, rows_here)
    col_map = lax.dynamic_slice_in_dim(own_map, col_index * cols_here, cols_here)
    row_keys = row_map // parent_rows * rows_here + jnp.arange(rows_here, dtype=jnp.int32)
    col_keys = col_map // parent_cols * cols_here + jnp.arange(cols_here, dtype=jnp.int32)
    sorted_block = update[jnp.argsort(row_keys)][:, jnp.argsort(col_keys)]
    part_rows = rows_here // n_row
    part_cols = cols_here // (2 * n_col)
    pieces = (
        sorted_block.reshape(n_row, part_rows, 2, n_col, part_cols)
        .transpose(2, 0, 3, 1, 4)
        .reshape(-1, part_cols)
    )
    arrived = lax.all_to_all(
        pieces, ("child", "row", "col"), split_axis=0, concat_axis=0, tiled=True
    )
    arrived = (
        arrived.reshape(2, n_row, n_col, part_rows, part_cols)
        .transpose(0, 1, 3, 2, 4)
        .reshape(2, rows_here, n_col * part_cols)
    )
    col_owner = child_index * n_col + col_index
    assembled = parent_front
    for source in range(2):
        parent_map = index_maps[source]
        row_slots = select_rows(parent_map, row_index, parent_rows, rows_here)
        col_slots = select_rows(parent_map, col_owner, parent_cols, n_col * part_cols)
        row_lookup = invert_slots(row_slots, parent_rows)
        col_lookup = invert_slots(col_slots, parent_cols)
        padded = jnp.pad(arrived[source], ((0, 1), (0, 1)))
        placed = jnp.take(jnp.take(padded, row_lookup, axis=0), col_lookup, axis=1)
        assembled = assembled + placed
    return (assembled, own_panel[None])


def solution(mesh):
    in_specs = (P("child", "row", "col"), P("row", ("child", "col")), P(), P())
    out_specs = (P("row", ("child", "col")), P("child", "row", None))
    return jax.shard_map(
        on_device, mesh=mesh, in_specs=in_specs, out_specs=out_specs, check_vma=False
    )
```

```python
import jax
import jax.numpy as jnp
from jax import lax
from jax.sharding import PartitionSpec as P

PANEL = 512
FRONT = 8192


def from_root(value, axis, source):
    kept = jnp.where(lax.axis_index(axis) == source, value, 0).astype(value.dtype)
    return lax.psum(kept, axis)


def spread_sum(value, axis):
    count = lax.axis_size(axis)
    pieces = value.reshape(count, value.shape[0] // count, value.shape[1])
    arrived = lax.all_to_all(pieces, axis, 0, 0, tiled=True)
    return lax.all_gather(arrived.sum(0), axis, axis=0, tiled=True)


def from_first(value, axis):
    count = lax.axis_size(axis)
    pieces = value.reshape(count, value.shape[0] // count, value.shape[1])
    arrived = lax.all_to_all(pieces, axis, 0, 0, tiled=True)
    return lax.all_gather(arrived[0], axis, axis=0, tiled=True)


def select_rows(parent_map, owner, width, count):
    everywhere = jnp.arange(FRONT, dtype=jnp.int32)
    keyed = jnp.where(parent_map // width == owner, everywhere, everywhere + FRONT)
    chosen = jnp.argsort(keyed)[:count]
    return parent_map[chosen] - owner * width


def invert_slots(slots, length):
    count = slots.shape[0]
    lookup = jnp.full((length,), count, jnp.int32)
    return lookup.at[slots].set(jnp.arange(count, dtype=jnp.int32))


def one_hot(order, size):
    positions = jnp.arange(size, dtype=jnp.int32)
    return (positions[:, None] == order[None, :]).astype(jnp.float32)


def exact_matmul(values, select):
    return jnp.dot(values, select, precision=lax.Precision.HIGHEST)


def factor_panel(diag_factor, inverse, columns, global_rows, own_order):
    solved = jnp.dot(columns, inverse.T, precision=lax.Precision.HIGHEST)
    top_rows = jnp.pad(diag_factor, ((0, columns.shape[0] - PANEL), (0, 0)))
    result = jnp.where(global_rows[:, None] < PANEL, top_rows, solved)
    return jnp.where(global_rows[:, None] < own_order, result, jnp.float32(0.0))


def on_device(child_fronts, parent_front, index_maps, orders):
    block_here = child_fronts[0]
    rows_here, cols_here = block_here.shape
    child_index = lax.axis_index("child")
    row_index = lax.axis_index("row")
    col_index = lax.axis_index("col")
    n_row = lax.axis_size("row")
    n_col = lax.axis_size("col")
    own_map = lax.dynamic_index_in_dim(index_maps, child_index, 0, keepdims=False)
    own_order = lax.dynamic_index_in_dim(orders, child_index, 0, keepdims=False)
    global_rows = row_index * rows_here + jnp.arange(rows_here, dtype=jnp.int32)
    global_cols = col_index * cols_here + jnp.arange(cols_here, dtype=jnp.int32)
    columns = from_first(block_here[:, :PANEL], "col")
    sent = jnp.concatenate(
        [
            jnp.where(row_index == col_index, columns, 0),
            jnp.where(row_index == 0, columns[:PANEL], 0),
        ]
    )
    received = spread_sum(sent, "row")
    other_columns, corner = received[:rows_here], received[rows_here:]
    diag_factor = jnp.linalg.cholesky(corner)
    inverse = lax.linalg.triangular_solve(
        diag_factor, jnp.eye(PANEL, dtype=jnp.float32), left_side=True, lower=True
    )
    own_panel = factor_panel(diag_factor, inverse, columns, global_rows, own_order)
    other_panel = factor_panel(diag_factor, inverse, other_columns, global_cols, own_order)
    update = block_here - jnp.dot(own_panel, other_panel.T, precision=lax.Precision.HIGHEST)
    live_rows = (global_rows >= PANEL) & (global_rows < own_order)
    live_cols = (global_cols >= PANEL) & (global_cols < own_order)
    update = jnp.where(live_rows[:, None] & live_cols[None, :], update, jnp.float32(0.0))
    parent_rows, parent_cols = parent_front.shape
    row_map = lax.dynamic_slice_in_dim(own_map, row_index * rows_here, rows_here)
    col_map = lax.dynamic_slice_in_dim(own_map, col_index * cols_here, cols_here)
    row_keys = row_map // parent_rows * rows_here + jnp.arange(rows_here, dtype=jnp.int32)
    col_keys = col_map // parent_cols * cols_here + jnp.arange(cols_here, dtype=jnp.int32)
    col_order = jnp.argsort(col_keys)
    col_select = one_hot(col_order, cols_here)
    sorted_block = exact_matmul(update[jnp.argsort(row_keys)], col_select)
    part_rows = rows_here // n_row
    part_cols = cols_here // (2 * n_col)
    pieces = (
        sorted_block.reshape(n_row, part_rows, 2, n_col, part_cols)
        .transpose(2, 0, 3, 1, 4)
        .reshape(-1, part_cols)
    )
    arrived = lax.all_to_all(
        pieces, ("child", "row", "col"), split_axis=0, concat_axis=0, tiled=True
    )
    arrived = (
        arrived.reshape(2, n_row, n_col, part_rows, part_cols)
        .transpose(0, 1, 3, 2, 4)
        .reshape(2, rows_here, n_col * part_cols)
    )
    col_owner = child_index * n_col + col_index
    placed_rows = []
    col_selects = []
    for source in range(2):
        parent_map = index_maps[source]
        row_slots = select_rows(parent_map, row_index, parent_rows, rows_here)
        col_slots = select_rows(parent_map, col_owner, parent_cols, n_col * part_cols)
        row_lookup = invert_slots(row_slots, parent_rows)
        padded = jnp.pad(arrived[source], ((0, 1), (0, 0)))
        placed_rows.append(jnp.take(padded, row_lookup, axis=0))
        col_selects.append(one_hot(col_slots, parent_cols).T)
    placed = exact_matmul(
        jnp.concatenate(placed_rows, axis=1), jnp.concatenate(col_selects, axis=0)
    )
    assembled = parent_front + placed
    return (assembled, own_panel[None])


def solution(mesh):
    in_specs = (P("child", "row", "col"), P("row", ("child", "col")), P(), P())
    out_specs = (P("row", ("child", "col")), P("child", "row", None))
    return jax.shard_map(
        on_device, mesh=mesh, in_specs=in_specs, out_specs=out_specs, check_vma=False
    )
```

```python
import jax
import jax.numpy as jnp
from jax import lax
from jax.sharding import PartitionSpec as P

PANEL = 512
FRONT = 8192


def from_root(value, axis, source):
    kept = jnp.where(lax.axis_index(axis) == source, value, 0).astype(value.dtype)
    return lax.psum(kept, axis)


def spread_sum(value, axis):
    count = lax.axis_size(axis)
    pieces = value.reshape(count, value.shape[0] // count, value.shape[1])
    arrived = lax.all_to_all(pieces, axis, 0, 0, tiled=True)
    return lax.all_gather(arrived.sum(0), axis, axis=0, tiled=True)


def from_first(value, axis):
    count = lax.axis_size(axis)
    pieces = value.reshape(count, value.shape[0] // count, value.shape[1])
    arrived = lax.all_to_all(pieces, axis, 0, 0, tiled=True)
    return lax.all_gather(arrived[0], axis, axis=0, tiled=True)


def select_rows(parent_map, owner, width, count):
    everywhere = jnp.arange(FRONT, dtype=jnp.int32)
    keyed = jnp.where(parent_map // width == owner, everywhere, everywhere + FRONT)
    chosen = jnp.argsort(keyed)[:count]
    return parent_map[chosen] - owner * width


def invert_slots(slots, length):
    count = slots.shape[0]
    lookup = jnp.full((length,), count, jnp.int32)
    return lookup.at[slots].set(jnp.arange(count, dtype=jnp.int32))


def one_hot(order, size):
    positions = jnp.arange(size, dtype=jnp.int32)
    return (positions[:, None] == order[None, :]).astype(jnp.float32)


def exact_matmul(values, select):
    return jnp.dot(values, select, precision=lax.Precision.HIGHEST)


def factor_panel(diag_factor, inverse, columns, global_rows, own_order):
    solved = jnp.dot(columns, inverse.T, precision=lax.Precision.HIGHEST)
    top_rows = jnp.pad(diag_factor, ((0, columns.shape[0] - PANEL), (0, 0)))
    result = jnp.where(global_rows[:, None] < PANEL, top_rows, solved)
    return jnp.where(global_rows[:, None] < own_order, result, jnp.float32(0.0))


def on_device(child_fronts, parent_front, index_maps, orders):
    block_here = child_fronts[0]
    rows_here, cols_here = block_here.shape
    child_index = lax.axis_index("child")
    row_index = lax.axis_index("row")
    col_index = lax.axis_index("col")
    n_row = lax.axis_size("row")
    n_col = lax.axis_size("col")
    own_map = lax.dynamic_index_in_dim(index_maps, child_index, 0, keepdims=False)
    own_order = lax.dynamic_index_in_dim(orders, child_index, 0, keepdims=False)
    global_rows = row_index * rows_here + jnp.arange(rows_here, dtype=jnp.int32)
    global_cols = col_index * cols_here + jnp.arange(cols_here, dtype=jnp.int32)
    columns = from_first(block_here[:, :PANEL], "col")
    sent = jnp.concatenate(
        [
            jnp.where(row_index == col_index, columns, 0),
            jnp.where(row_index == 0, columns[:PANEL], 0),
        ]
    )
    received = spread_sum(sent, "row")
    other_columns, corner = received[:rows_here], received[rows_here:]
    parent_rows, parent_cols = parent_front.shape
    row_map = lax.dynamic_slice_in_dim(own_map, row_index * rows_here, rows_here)
    col_map = lax.dynamic_slice_in_dim(own_map, col_index * cols_here, cols_here)
    row_keys = row_map // parent_rows * rows_here + jnp.arange(rows_here, dtype=jnp.int32)
    col_keys = col_map // parent_cols * cols_here + jnp.arange(cols_here, dtype=jnp.int32)
    col_order = jnp.argsort(col_keys)
    row_order = jnp.argsort(row_keys)
    col_select = one_hot(col_order, cols_here)
    part_cols = cols_here // (2 * n_col)
    col_owner = child_index * n_col + col_index
    row_lookups = []
    col_selects = []
    for source in range(2):
        parent_map = index_maps[source]
        row_slots = select_rows(parent_map, row_index, parent_rows, rows_here)
        col_slots = select_rows(parent_map, col_owner, parent_cols, n_col * part_cols)
        row_lookups.append(invert_slots(row_slots, parent_rows))
        col_selects.append(one_hot(col_slots, parent_cols).T)
    parent_select = jnp.concatenate(col_selects, axis=0)
    corner, row_order, col_select, row_lookups, parent_select = lax.optimization_barrier(
        (corner, row_order, col_select, row_lookups, parent_select)
    )
    diag_factor = jnp.linalg.cholesky(corner)
    inverse = lax.linalg.triangular_solve(
        diag_factor, jnp.eye(PANEL, dtype=jnp.float32), left_side=True, lower=True
    )
    own_panel = factor_panel(diag_factor, inverse, columns, global_rows, own_order)
    other_panel = factor_panel(diag_factor, inverse, other_columns, global_cols, own_order)
    update = block_here - jnp.dot(own_panel, other_panel.T, precision=lax.Precision.HIGHEST)
    live_rows = (global_rows >= PANEL) & (global_rows < own_order)
    live_cols = (global_cols >= PANEL) & (global_cols < own_order)
    update = jnp.where(live_rows[:, None] & live_cols[None, :], update, jnp.float32(0.0))
    sorted_block = exact_matmul(update[row_order], col_select)
    part_rows = rows_here // n_row
    part_cols = cols_here // (2 * n_col)
    pieces = (
        sorted_block.reshape(n_row, part_rows, 2, n_col, part_cols)
        .transpose(2, 0, 3, 1, 4)
        .reshape(-1, part_cols)
    )
    arrived = lax.all_to_all(
        pieces, ("child", "row", "col"), split_axis=0, concat_axis=0, tiled=True
    )
    arrived = (
        arrived.reshape(2, n_row, n_col, part_rows, part_cols)
        .transpose(0, 1, 3, 2, 4)
        .reshape(2, rows_here, n_col * part_cols)
    )
    placed_rows = []
    for source in range(2):
        padded = jnp.pad(arrived[source], ((0, 1), (0, 0)))
        placed_rows.append(jnp.take(padded, row_lookups[source], axis=0))
    placed = exact_matmul(
        jnp.concatenate(placed_rows, axis=1), parent_select
    )
    assembled = parent_front + placed
    return (assembled, own_panel[None])


def solution(mesh):
    in_specs = (P("child", "row", "col"), P("row", ("child", "col")), P(), P())
    out_specs = (P("row", ("child", "col")), P("child", "row", None))
    return jax.shard_map(
        on_device, mesh=mesh, in_specs=in_specs, out_specs=out_specs, check_vma=False
    )
```

```python
import jax
import jax.numpy as jnp
from jax import lax
from jax.sharding import PartitionSpec as P

PANEL = 512
FRONT = 8192


def from_root(value, axis, source):
    kept = jnp.where(lax.axis_index(axis) == source, value, 0).astype(value.dtype)
    return lax.psum(kept, axis)


def spread_sum(value, axis):
    count = lax.axis_size(axis)
    pieces = value.reshape(count, value.shape[0] // count, value.shape[1])
    arrived = lax.all_to_all(pieces, axis, 0, 0, tiled=True)
    return lax.all_gather(arrived.sum(0), axis, axis=0, tiled=True)


def from_first(value, axis):
    count = lax.axis_size(axis)
    pieces = value.reshape(count, value.shape[0] // count, value.shape[1])
    arrived = lax.all_to_all(pieces, axis, 0, 0, tiled=True)
    return lax.all_gather(arrived[0], axis, axis=0, tiled=True)


def select_rows(parent_map, owner, width, count):
    everywhere = jnp.arange(FRONT, dtype=jnp.int32)
    keyed = jnp.where(parent_map // width == owner, everywhere, everywhere + FRONT)
    chosen = jnp.argsort(keyed)[:count]
    return parent_map[chosen] - owner * width


def invert_slots(slots, length):
    count = slots.shape[0]
    lookup = jnp.full((length,), count, jnp.int32)
    return lookup.at[slots].set(jnp.arange(count, dtype=jnp.int32))


def one_hot(order, size):
    positions = jnp.arange(size, dtype=jnp.int32)
    return (positions[:, None] == order[None, :]).astype(jnp.float32)


def exact_matmul(values, select):
    return jnp.dot(values, select, precision=lax.Precision.HIGHEST)


def factor_panel(diag_factor, inverse, columns, global_rows, own_order):
    solved = jnp.dot(columns, inverse.T, precision=lax.Precision.HIGHEST)
    top_rows = jnp.pad(diag_factor, ((0, columns.shape[0] - PANEL), (0, 0)))
    result = jnp.where(global_rows[:, None] < PANEL, top_rows, solved)
    return jnp.where(global_rows[:, None] < own_order, result, jnp.float32(0.0))


def on_device(child_fronts, parent_front, index_maps, orders):
    block_here = child_fronts[0]
    rows_here, cols_here = block_here.shape
    child_index = lax.axis_index("child")
    row_index = lax.axis_index("row")
    col_index = lax.axis_index("col")
    n_row = lax.axis_size("row")
    n_col = lax.axis_size("col")
    own_map = lax.dynamic_index_in_dim(index_maps, child_index, 0, keepdims=False)
    own_order = lax.dynamic_index_in_dim(orders, child_index, 0, keepdims=False)
    global_rows = row_index * rows_here + jnp.arange(rows_here, dtype=jnp.int32)
    global_cols = col_index * cols_here + jnp.arange(cols_here, dtype=jnp.int32)
    columns = from_first(block_here[:, :PANEL], "col")
    sent = jnp.concatenate(
        [
            jnp.where(row_index == col_index, columns, 0),
            jnp.where(row_index == 0, columns[:PANEL], 0),
        ]
    )
    received = spread_sum(sent, "row")
    other_columns, corner = received[:rows_here], received[rows_here:]
    diag_factor = jnp.linalg.cholesky(corner)
    inverse = lax.linalg.triangular_solve(
        diag_factor, jnp.eye(PANEL, dtype=jnp.float32), left_side=True, lower=True
    )
    own_panel = factor_panel(diag_factor, inverse, columns, global_rows, own_order)
    other_panel = factor_panel(diag_factor, inverse, other_columns, global_cols, own_order)
    update = block_here - jnp.dot(own_panel, other_panel.T, precision=lax.Precision.HIGHEST)
    live_rows = (global_rows >= PANEL) & (global_rows < own_order)
    live_cols = (global_cols >= PANEL) & (global_cols < own_order)
    update = jnp.where(live_rows[:, None] & live_cols[None, :], update, jnp.float32(0.0))
    parent_rows, parent_cols = parent_front.shape
    row_map = lax.dynamic_slice_in_dim(own_map, row_index * rows_here, rows_here)
    col_map = lax.dynamic_slice_in_dim(own_map, col_index * cols_here, cols_here)
    row_keys = row_map // parent_rows * rows_here + jnp.arange(rows_here, dtype=jnp.int32)
    col_keys = col_map // parent_cols * cols_here + jnp.arange(cols_here, dtype=jnp.int32)
    col_order = jnp.argsort(col_keys)
    col_select = one_hot(col_order, cols_here)
    turned = jnp.einsum(
        "qj,iq->ji", col_select, update[jnp.argsort(row_keys)],
        precision=lax.Precision.HIGHEST,
    )
    part_rows = rows_here // n_row
    part_cols = cols_here // (2 * n_col)
    pieces = (
        turned.reshape(2, n_col, part_cols, n_row, part_rows)
        .transpose(0, 3, 1, 2, 4)
        .reshape(-1, part_rows)
    )
    arrived = lax.all_to_all(
        pieces, ("child", "row", "col"), split_axis=0, concat_axis=0, tiled=True
    )
    arrived = (
        arrived.reshape(2, n_row, n_col, part_cols, part_rows)
        .transpose(0, 2, 3, 1, 4)
        .reshape(2, n_col * part_cols, rows_here)
    )
    col_owner = child_index * n_col + col_index
    assembled = parent_front
    for source in range(2):
        parent_map = index_maps[source]
        row_slots = select_rows(parent_map, row_index, parent_rows, rows_here)
        col_slots = select_rows(parent_map, col_owner, parent_cols, n_col * part_cols)
        row_lookup = invert_slots(row_slots, parent_rows)
        spread = jnp.einsum(
            "qi,pq->ip", arrived[source], one_hot(col_slots, parent_cols),
            precision=lax.Precision.HIGHEST,
        )
        padded = jnp.pad(spread, ((0, 1), (0, 0)))
        assembled = assembled + jnp.take(padded, row_lookup, axis=0)
    return (assembled, own_panel[None])


def solution(mesh):
    in_specs = (P("child", "row", "col"), P("row", ("child", "col")), P(), P())
    out_specs = (P("row", ("child", "col")), P("child", "row", None))
    return jax.shard_map(
        on_device, mesh=mesh, in_specs=in_specs, out_specs=out_specs, check_vma=False
    )
```

```python
import jax
import jax.numpy as jnp
from jax import lax
from jax.sharding import PartitionSpec as P

PANEL = 512
FRONT = 8192


def from_root(value, axis, source):
    kept = jnp.where(lax.axis_index(axis) == source, value, 0).astype(value.dtype)
    return lax.psum(kept, axis)


def spread_sum(value, axis):
    count = lax.axis_size(axis)
    pieces = value.reshape(count, value.shape[0] // count, value.shape[1])
    arrived = lax.all_to_all(pieces, axis, 0, 0, tiled=True)
    return lax.all_gather(arrived.sum(0), axis, axis=0, tiled=True)


def from_first(value, axis, gather=True):
    count = lax.axis_size(axis)
    pieces = value.reshape(count, value.shape[0] // count, value.shape[1])
    arrived = lax.all_to_all(pieces, axis, 0, 0, tiled=True)
    if not gather:
        return arrived[0]
    return lax.all_gather(arrived[0], axis, axis=0, tiled=True)


def select_rows(parent_map, owner, width, count):
    everywhere = jnp.arange(FRONT, dtype=jnp.int32)
    keyed = jnp.where(parent_map // width == owner, everywhere, everywhere + FRONT)
    chosen = jnp.argsort(keyed)[:count]
    return parent_map[chosen] - owner * width


def invert_slots(slots, length):
    count = slots.shape[0]
    lookup = jnp.full((length,), count, jnp.int32)
    return lookup.at[slots].set(jnp.arange(count, dtype=jnp.int32))


def one_hot(order, size):
    positions = jnp.arange(size, dtype=jnp.int32)
    return (positions[:, None] == order[None, :]).astype(jnp.float32)


def exact_matmul(values, select):
    return jnp.dot(values, select, precision=lax.Precision.HIGHEST)


def factor_panel(diag_factor, inverse, columns, global_rows, own_order):
    solved = jnp.dot(columns, inverse.T, precision=lax.Precision.HIGHEST)
    top_rows = jnp.pad(diag_factor, ((0, columns.shape[0] - PANEL), (0, 0)))
    result = jnp.where(global_rows[:, None] < PANEL, top_rows, solved)
    return jnp.where(global_rows[:, None] < own_order, result, jnp.float32(0.0))


def on_device(child_fronts, parent_front, index_maps, orders):
    block_here = child_fronts[0]
    rows_here, cols_here = block_here.shape
    child_index = lax.axis_index("child")
    row_index = lax.axis_index("row")
    col_index = lax.axis_index("col")
    n_row = lax.axis_size("row")
    n_col = lax.axis_size("col")
    own_map = lax.dynamic_index_in_dim(index_maps, child_index, 0, keepdims=False)
    own_order = lax.dynamic_index_in_dim(orders, child_index, 0, keepdims=False)
    global_rows = row_index * rows_here + jnp.arange(rows_here, dtype=jnp.int32)
    global_cols = col_index * cols_here + jnp.arange(cols_here, dtype=jnp.int32)
    panel_here = block_here[:, :PANEL]
    part_rows = rows_here // n_row
    flat = n_col * row_index + col_index
    transposed_piece = jnp.zeros((part_rows, PANEL), jnp.float32)
    for target in range(n_row):
        piece = panel_here[target * part_rows:(target + 1) * part_rows]
        pairs = [(n_col * k, n_col * target + k) for k in range(n_col)]
        moved = lax.ppermute(piece, ("row", "col"), [p for p in pairs if p[0] != p[1]])
        if target == 0:
            moved = jnp.where(flat == 0, piece, moved)
        transposed_piece = jnp.where(row_index == target, moved, transposed_piece)
    columns = from_first(panel_here, "col")
    corner_piece = from_first(columns[:PANEL], "row", gather=False)
    gathered = lax.all_gather(
        jnp.concatenate([transposed_piece, corner_piece]), "row", axis=0, tiled=False
    )
    other_columns = gathered[:, :part_rows].reshape(rows_here, PANEL)
    corner = gathered[:, part_rows:].reshape(PANEL, PANEL)
    diag_factor = jnp.linalg.cholesky(corner)
    inverse = lax.linalg.triangular_solve(
        diag_factor, jnp.eye(PANEL, dtype=jnp.float32), left_side=True, lower=True
    )
    own_panel = factor_panel(diag_factor, inverse, columns, global_rows, own_order)
    other_panel = factor_panel(diag_factor, inverse, other_columns, global_cols, own_order)
    update = block_here - jnp.dot(own_panel, other_panel.T, precision=lax.Precision.HIGHEST)
    live_rows = (global_rows >= PANEL) & (global_rows < own_order)
    live_cols = (global_cols >= PANEL) & (global_cols < own_order)
    update = jnp.where(live_rows[:, None] & live_cols[None, :], update, jnp.float32(0.0))
    parent_rows, parent_cols = parent_front.shape
    row_map = lax.dynamic_slice_in_dim(own_map, row_index * rows_here, rows_here)
    col_map = lax.dynamic_slice_in_dim(own_map, col_index * cols_here, cols_here)
    row_keys = row_map // parent_rows * rows_here + jnp.arange(rows_here, dtype=jnp.int32)
    col_keys = col_map // parent_cols * cols_here + jnp.arange(cols_here, dtype=jnp.int32)
    col_order = jnp.argsort(col_keys)
    col_select = one_hot(col_order, cols_here)
    turned = jnp.einsum(
        "qj,iq->ji", col_select, update[jnp.argsort(row_keys)],
        precision=lax.Precision.HIGHEST,
    )
    part_cols = cols_here // (2 * n_col)
    pieces = (
        turned.reshape(2, n_col, part_cols, n_row, part_rows)
        .transpose(0, 3, 1, 2, 4)
        .reshape(-1, part_rows)
    )
    arrived = lax.all_to_all(
        pieces, ("child", "row", "col"), split_axis=0, concat_axis=0, tiled=True
    )
    arrived = (
        arrived.reshape(2, n_row, n_col, part_cols, part_rows)
        .transpose(0, 2, 3, 1, 4)
        .reshape(2, n_col * part_cols, rows_here)
    )
    col_owner = child_index * n_col + col_index
    assembled = parent_front
    for source in range(2):
        parent_map = index_maps[source]
        row_slots = select_rows(parent_map, row_index, parent_rows, rows_here)
        col_slots = select_rows(parent_map, col_owner, parent_cols, n_col * part_cols)
        row_lookup = invert_slots(row_slots, parent_rows)
        spread = jnp.einsum(
            "qi,pq->ip", arrived[source], one_hot(col_slots, parent_cols),
            precision=lax.Precision.HIGHEST,
        )
        padded = jnp.pad(spread, ((0, 1), (0, 0)))
        assembled = assembled + jnp.take(padded, row_lookup, axis=0)
    return (assembled, own_panel[None])


def solution(mesh):
    in_specs = (P("child", "row", "col"), P("row", ("child", "col")), P(), P())
    out_specs = (P("row", ("child", "col")), P("child", "row", None))
    return jax.shard_map(
        on_device, mesh=mesh, in_specs=in_specs, out_specs=out_specs, check_vma=False
    )
```

```python
import jax
import jax.numpy as jnp
from jax import lax
from jax.sharding import PartitionSpec as P

PANEL = 512
FRONT = 8192


def from_root(value, axis, source):
    kept = jnp.where(lax.axis_index(axis) == source, value, 0).astype(value.dtype)
    return lax.psum(kept, axis)


def spread_sum(value, axis):
    count = lax.axis_size(axis)
    pieces = value.reshape(count, value.shape[0] // count, value.shape[1])
    arrived = lax.all_to_all(pieces, axis, 0, 0, tiled=True)
    return lax.all_gather(arrived.sum(0), axis, axis=0, tiled=True)


def from_first(value, axis):
    count = lax.axis_size(axis)
    pieces = value.reshape(count, value.shape[0] // count, value.shape[1])
    arrived = lax.all_to_all(pieces, axis, 0, 0, tiled=True)
    return lax.all_gather(arrived[0], axis, axis=0, tiled=True)


def select_rows(parent_map, owner, width, count):
    everywhere = jnp.arange(FRONT, dtype=jnp.int32)
    keyed = jnp.where(parent_map // width == owner, everywhere, everywhere + FRONT)
    chosen = jnp.argsort(keyed)[:count]
    return parent_map[chosen] - owner * width


def invert_slots(slots, length):
    count = slots.shape[0]
    lookup = jnp.full((length,), count, jnp.int32)
    return lookup.at[slots].set(jnp.arange(count, dtype=jnp.int32))


def one_hot(order, size):
    positions = jnp.arange(size, dtype=jnp.int32)
    return (positions[:, None] == order[None, :]).astype(jnp.float32)


def exact_matmul(values, select):
    return jnp.dot(values, select, precision=lax.Precision.HIGHEST)


def blocked_inverse(lower, size):
    count = lower.shape[0] // size
    part = lambda m, i, j: m[i * size:(i + 1) * size, j * size:(j + 1) * size]
    blocks = {}
    for i in range(count):
        blocks[i, i] = lax.linalg.triangular_solve(
            part(lower, i, i), jnp.eye(size, dtype=jnp.float32), left_side=True, lower=True
        )
    for i in range(count):
        for j in range(i - 1, -1, -1):
            total = sum(
                jnp.dot(part(lower, i, k), blocks[k, j], precision=lax.Precision.HIGHEST)
                for k in range(j, i)
            )
            blocks[i, j] = -jnp.dot(blocks[i, i], total, precision=lax.Precision.HIGHEST)
    zero = jnp.zeros((size, size), jnp.float32)
    return jnp.concatenate(
        [
            jnp.concatenate([blocks[i, j] if j <= i else zero for j in range(count)], axis=1)
            for i in range(count)
        ]
    )


def factor_panel(diag_factor, inverse, columns, global_rows, own_order):
    solved = jnp.dot(columns, inverse.T, precision=lax.Precision.HIGHEST)
    top_rows = jnp.pad(diag_factor, ((0, columns.shape[0] - PANEL), (0, 0)))
    result = jnp.where(global_rows[:, None] < PANEL, top_rows, solved)
    return jnp.where(global_rows[:, None] < own_order, result, jnp.float32(0.0))


def on_device(child_fronts, parent_front, index_maps, orders):
    block_here = child_fronts[0]
    rows_here, cols_here = block_here.shape
    child_index = lax.axis_index("child")
    row_index = lax.axis_index("row")
    col_index = lax.axis_index("col")
    n_row = lax.axis_size("row")
    n_col = lax.axis_size("col")
    own_map = lax.dynamic_index_in_dim(index_maps, child_index, 0, keepdims=False)
    own_order = lax.dynamic_index_in_dim(orders, child_index, 0, keepdims=False)
    global_rows = row_index * rows_here + jnp.arange(rows_here, dtype=jnp.int32)
    global_cols = col_index * cols_here + jnp.arange(cols_here, dtype=jnp.int32)
    columns = from_first(block_here[:, :PANEL], "col")
    sent = jnp.concatenate(
        [
            jnp.where(row_index == col_index, columns, 0),
            jnp.where(row_index == 0, columns[:PANEL], 0),
        ]
    )
    received = spread_sum(sent, "row")
    other_columns, corner = received[:rows_here], received[rows_here:]
    diag_factor = jnp.linalg.cholesky(corner)
    inverse = blocked_inverse(diag_factor, PANEL // 4)
    own_panel = factor_panel(diag_factor, inverse, columns, global_rows, own_order)
    other_panel = factor_panel(diag_factor, inverse, other_columns, global_cols, own_order)
    update = block_here - jnp.dot(own_panel, other_panel.T, precision=lax.Precision.HIGHEST)
    live_rows = (global_rows >= PANEL) & (global_rows < own_order)
    live_cols = (global_cols >= PANEL) & (global_cols < own_order)
    update = jnp.where(live_rows[:, None] & live_cols[None, :], update, jnp.float32(0.0))
    parent_rows, parent_cols = parent_front.shape
    row_map = lax.dynamic_slice_in_dim(own_map, row_index * rows_here, rows_here)
    col_map = lax.dynamic_slice_in_dim(own_map, col_index * cols_here, cols_here)
    row_keys = row_map // parent_rows * rows_here + jnp.arange(rows_here, dtype=jnp.int32)
    col_keys = col_map // parent_cols * cols_here + jnp.arange(cols_here, dtype=jnp.int32)
    col_order = jnp.argsort(col_keys)
    col_select = one_hot(col_order, cols_here)
    turned = jnp.einsum(
        "qj,iq->ji", col_select, update[jnp.argsort(row_keys)],
        precision=lax.Precision.HIGHEST,
    )
    part_rows = rows_here // n_row
    part_cols = cols_here // (2 * n_col)
    pieces = (
        turned.reshape(2, n_col, part_cols, n_row, part_rows)
        .transpose(0, 3, 1, 2, 4)
        .reshape(-1, part_rows)
    )
    arrived = lax.all_to_all(
        pieces, ("child", "row", "col"), split_axis=0, concat_axis=0, tiled=True
    )
    arrived = (
        arrived.reshape(2, n_row, n_col, part_cols, part_rows)
        .transpose(0, 2, 3, 1, 4)
        .reshape(2, n_col * part_cols, rows_here)
    )
    col_owner = child_index * n_col + col_index
    assembled = parent_front
    for source in range(2):
        parent_map = index_maps[source]
        row_slots = select_rows(parent_map, row_index, parent_rows, rows_here)
        col_slots = select_rows(parent_map, col_owner, parent_cols, n_col * part_cols)
        row_lookup = invert_slots(row_slots, parent_rows)
        spread = jnp.einsum(
            "qi,pq->ip", arrived[source], one_hot(col_slots, parent_cols),
            precision=lax.Precision.HIGHEST,
        )
        padded = jnp.pad(spread, ((0, 1), (0, 0)))
        assembled = assembled + jnp.take(padded, row_lookup, axis=0)
    return (assembled, own_panel[None])


def solution(mesh):
    in_specs = (P("child", "row", "col"), P("row", ("child", "col")), P(), P())
    out_specs = (P("row", ("child", "col")), P("child", "row", None))
    return jax.shard_map(
        on_device, mesh=mesh, in_specs=in_specs, out_specs=out_specs, check_vma=False
    )
```

```python
import jax
import jax.numpy as jnp
from jax import lax
from jax.sharding import PartitionSpec as P

PANEL = 512
FRONT = 8192


def from_root(value, axis, source):
    kept = jnp.where(lax.axis_index(axis) == source, value, 0).astype(value.dtype)
    return lax.psum(kept, axis)


def spread_sum(value, axis):
    count = lax.axis_size(axis)
    pieces = value.reshape(count, value.shape[0] // count, value.shape[1])
    arrived = lax.all_to_all(pieces, axis, 0, 0, tiled=True)
    return lax.all_gather(arrived.sum(0), axis, axis=0, tiled=True)


def from_first(value, axis):
    count = lax.axis_size(axis)
    pieces = value.reshape(count, value.shape[0] // count, value.shape[1])
    arrived = lax.all_to_all(pieces, axis, 0, 0, tiled=True)
    return lax.all_gather(arrived[0], axis, axis=0, tiled=True)


def select_rows(parent_map, owner, width, count):
    everywhere = jnp.arange(FRONT, dtype=jnp.int32)
    keyed = jnp.where(parent_map // width == owner, everywhere, everywhere + FRONT)
    chosen = jnp.argsort(keyed)[:count]
    return parent_map[chosen] - owner * width


def invert_slots(slots, length):
    count = slots.shape[0]
    lookup = jnp.full((length,), count, jnp.int32)
    return lookup.at[slots].set(jnp.arange(count, dtype=jnp.int32))


def one_hot(order, size):
    positions = jnp.arange(size, dtype=jnp.int32)
    return (positions[:, None] == order[None, :]).astype(jnp.float32)


def exact_matmul(values, select):
    return jnp.dot(values, select, precision=lax.Precision.HIGHEST)


def factor_and_invert(matrix, size):
    count = matrix.shape[0] // size
    eye = jnp.eye(size, dtype=jnp.float32)
    high = lax.Precision.HIGHEST
    trailing = (matrix + matrix.T) * 0.5
    factor, inverse = {}, {}
    for k in range(count):
        factor[k, k] = jnp.linalg.cholesky(trailing[:size, :size])
        inverse[k, k] = lax.linalg.triangular_solve(
            factor[k, k], eye, left_side=True, lower=True
        )
        if k + 1 < count:
            panel = jnp.dot(trailing[size:, :size], inverse[k, k].T, precision=high)
            for i in range(k + 1, count):
                factor[i, k] = panel[(i - k - 1) * size:(i - k) * size]
            trailing = trailing[size:, size:] - jnp.dot(panel, panel.T, precision=high)
    for i in range(count):
        for j in range(i - 1, -1, -1):
            total = sum(
                jnp.dot(factor[i, k], inverse[k, j], precision=high) for k in range(j, i)
            )
            inverse[i, j] = -jnp.dot(inverse[i, i], total, precision=high)
    zero = jnp.zeros((size, size), jnp.float32)

    def assemble(blocks):
        return jnp.concatenate(
            [
                jnp.concatenate(
                    [blocks[i, j] if j <= i else zero for j in range(count)], axis=1
                )
                for i in range(count)
            ]
        )

    return assemble(factor), assemble(inverse)


def factor_panel(diag_factor, inverse, columns, global_rows, own_order):
    solved = jnp.dot(columns, inverse.T, precision=lax.Precision.HIGHEST)
    top_rows = jnp.pad(diag_factor, ((0, columns.shape[0] - PANEL), (0, 0)))
    result = jnp.where(global_rows[:, None] < PANEL, top_rows, solved)
    return jnp.where(global_rows[:, None] < own_order, result, jnp.float32(0.0))


def on_device(child_fronts, parent_front, index_maps, orders):
    block_here = child_fronts[0]
    rows_here, cols_here = block_here.shape
    child_index = lax.axis_index("child")
    row_index = lax.axis_index("row")
    col_index = lax.axis_index("col")
    n_row = lax.axis_size("row")
    n_col = lax.axis_size("col")
    own_map = lax.dynamic_index_in_dim(index_maps, child_index, 0, keepdims=False)
    own_order = lax.dynamic_index_in_dim(orders, child_index, 0, keepdims=False)
    global_rows = row_index * rows_here + jnp.arange(rows_here, dtype=jnp.int32)
    global_cols = col_index * cols_here + jnp.arange(cols_here, dtype=jnp.int32)
    columns = from_first(block_here[:, :PANEL], "col")
    sent = jnp.concatenate(
        [
            jnp.where(row_index == col_index, columns, 0),
            jnp.where(row_index == 0, columns[:PANEL], 0),
        ]
    )
    received = spread_sum(sent, "row")
    other_columns, corner = received[:rows_here], received[rows_here:]
    diag_factor, inverse = factor_and_invert(corner, PANEL // 4)
    own_panel = factor_panel(diag_factor, inverse, columns, global_rows, own_order)
    other_panel = factor_panel(diag_factor, inverse, other_columns, global_cols, own_order)
    update = block_here - jnp.dot(own_panel, other_panel.T, precision=lax.Precision.HIGHEST)
    live_rows = (global_rows >= PANEL) & (global_rows < own_order)
    live_cols = (global_cols >= PANEL) & (global_cols < own_order)
    update = jnp.where(live_rows[:, None] & live_cols[None, :], update, jnp.float32(0.0))
    parent_rows, parent_cols = parent_front.shape
    row_map = lax.dynamic_slice_in_dim(own_map, row_index * rows_here, rows_here)
    col_map = lax.dynamic_slice_in_dim(own_map, col_index * cols_here, cols_here)
    row_keys = row_map // parent_rows * rows_here + jnp.arange(rows_here, dtype=jnp.int32)
    col_keys = col_map // parent_cols * cols_here + jnp.arange(cols_here, dtype=jnp.int32)
    col_order = jnp.argsort(col_keys)
    col_select = one_hot(col_order, cols_here)
    turned = jnp.einsum(
        "qj,iq->ji", col_select, update[jnp.argsort(row_keys)],
        precision=lax.Precision.HIGHEST,
    )
    part_rows = rows_here // n_row
    part_cols = cols_here // (2 * n_col)
    pieces = (
        turned.reshape(2, n_col, part_cols, n_row, part_rows)
        .transpose(0, 3, 1, 2, 4)
        .reshape(-1, part_rows)
    )
    arrived = lax.all_to_all(
        pieces, ("child", "row", "col"), split_axis=0, concat_axis=0, tiled=True
    )
    arrived = (
        arrived.reshape(2, n_row, n_col, part_cols, part_rows)
        .transpose(0, 2, 3, 1, 4)
        .reshape(2, n_col * part_cols, rows_here)
    )
    col_owner = child_index * n_col + col_index
    assembled = parent_front
    for source in range(2):
        parent_map = index_maps[source]
        row_slots = select_rows(parent_map, row_index, parent_rows, rows_here)
        col_slots = select_rows(parent_map, col_owner, parent_cols, n_col * part_cols)
        row_lookup = invert_slots(row_slots, parent_rows)
        spread = jnp.einsum(
            "qi,pq->ip", arrived[source], one_hot(col_slots, parent_cols),
            precision=lax.Precision.HIGHEST,
        )
        padded = jnp.pad(spread, ((0, 1), (0, 0)))
        assembled = assembled + jnp.take(padded, row_lookup, axis=0)
    return (assembled, own_panel[None])


def solution(mesh):
    in_specs = (P("child", "row", "col"), P("row", ("child", "col")), P(), P())
    out_specs = (P("row", ("child", "col")), P("child", "row", None))
    return jax.shard_map(
        on_device, mesh=mesh, in_specs=in_specs, out_specs=out_specs, check_vma=False
    )
```

```python
import jax
import jax.numpy as jnp
from jax import lax
from jax.sharding import PartitionSpec as P

PANEL = 512
FRONT = 8192


def from_root(value, axis, source):
    kept = jnp.where(lax.axis_index(axis) == source, value, 0).astype(value.dtype)
    return lax.psum(kept, axis)


def spread_sum(value, axis):
    count = lax.axis_size(axis)
    pieces = value.reshape(count, value.shape[0] // count, value.shape[1])
    arrived = lax.all_to_all(pieces, axis, 0, 0, tiled=True)
    return lax.all_gather(arrived.sum(0), axis, axis=0, tiled=True)


def from_first(value, axis):
    count = lax.axis_size(axis)
    pieces = value.reshape(count, value.shape[0] // count, value.shape[1])
    arrived = lax.all_to_all(pieces, axis, 0, 0, tiled=True)
    return lax.all_gather(arrived[0], axis, axis=0, tiled=True)


def select_rows(parent_map, owner, width, count):
    everywhere = jnp.arange(FRONT, dtype=jnp.int32)
    keyed = jnp.where(parent_map // width == owner, everywhere, everywhere + FRONT)
    chosen = jnp.argsort(keyed)[:count]
    return parent_map[chosen] - owner * width


def invert_slots(slots, length):
    count = slots.shape[0]
    lookup = jnp.full((length,), count, jnp.int32)
    return lookup.at[slots].set(jnp.arange(count, dtype=jnp.int32))


def one_hot(order, size):
    positions = jnp.arange(size, dtype=jnp.int32)
    return (positions[:, None] == order[None, :]).astype(jnp.float32)


def exact_matmul(values, select):
    return jnp.dot(values, select, precision=lax.Precision.HIGHEST)


def factor_and_invert(matrix, size):
    count = matrix.shape[0] // size
    eye = jnp.eye(size, dtype=jnp.float32)
    high = lax.Precision.HIGHEST
    trailing = (matrix + matrix.T) * 0.5
    factor, inverse = {}, {}
    for k in range(count):
        factor[k, k] = jnp.linalg.cholesky(trailing[:size, :size])
        inverse[k, k] = lax.linalg.triangular_solve(
            factor[k, k], eye, left_side=True, lower=True
        )
        if k + 1 < count:
            panel = jnp.dot(trailing[size:, :size], inverse[k, k].T, precision=high)
            for i in range(k + 1, count):
                factor[i, k] = panel[(i - k - 1) * size:(i - k) * size]
            trailing = trailing[size:, size:] - jnp.dot(panel, panel.T, precision=high)
    for i in range(count):
        for j in range(i - 1, -1, -1):
            total = sum(
                jnp.dot(factor[i, k], inverse[k, j], precision=high) for k in range(j, i)
            )
            inverse[i, j] = -jnp.dot(inverse[i, i], total, precision=high)
    zero = jnp.zeros((size, size), jnp.float32)

    def assemble(blocks):
        return jnp.concatenate(
            [
                jnp.concatenate(
                    [blocks[i, j] if j <= i else zero for j in range(count)], axis=1
                )
                for i in range(count)
            ]
        )

    return assemble(factor), assemble(inverse)


def factor_panel(diag_factor, inverse, columns, global_rows, own_order):
    solved = jnp.dot(columns, inverse.T, precision=lax.Precision.HIGHEST)
    top_rows = jnp.pad(diag_factor, ((0, columns.shape[0] - PANEL), (0, 0)))
    result = jnp.where(global_rows[:, None] < PANEL, top_rows, solved)
    return jnp.where(global_rows[:, None] < own_order, result, jnp.float32(0.0))


def on_device(child_fronts, parent_front, index_maps, orders):
    block_here = child_fronts[0]
    rows_here, cols_here = block_here.shape
    child_index = lax.axis_index("child")
    row_index = lax.axis_index("row")
    col_index = lax.axis_index("col")
    n_row = lax.axis_size("row")
    n_col = lax.axis_size("col")
    own_map = lax.dynamic_index_in_dim(index_maps, child_index, 0, keepdims=False)
    own_order = lax.dynamic_index_in_dim(orders, child_index, 0, keepdims=False)
    global_rows = row_index * rows_here + jnp.arange(rows_here, dtype=jnp.int32)
    global_cols = col_index * cols_here + jnp.arange(cols_here, dtype=jnp.int32)
    columns = from_first(block_here[:, :PANEL], "col")
    sent = jnp.concatenate(
        [
            jnp.where(row_index == col_index, columns, 0),
            jnp.where(row_index == 0, columns[:PANEL], 0),
        ]
    )
    received = spread_sum(sent, "row")
    other_columns, corner = received[:rows_here], received[rows_here:]
    parent_rows, parent_cols = parent_front.shape
    row_map = lax.dynamic_slice_in_dim(own_map, row_index * rows_here, rows_here)
    col_map = lax.dynamic_slice_in_dim(own_map, col_index * cols_here, cols_here)
    row_keys = row_map // parent_rows * rows_here + jnp.arange(rows_here, dtype=jnp.int32)
    col_keys = col_map // parent_cols * cols_here + jnp.arange(cols_here, dtype=jnp.int32)
    col_order = jnp.argsort(col_keys)
    row_order = jnp.argsort(row_keys)
    turned_block = jnp.einsum(
        "qj,iq->ji", one_hot(col_order, cols_here), block_here[row_order],
        precision=lax.Precision.HIGHEST,
    )
    diag_factor, inverse = factor_and_invert(corner, PANEL // 4)
    own_panel = factor_panel(diag_factor, inverse, columns, global_rows, own_order)
    high = lax.Precision.HIGHEST
    turned_panels = jnp.dot(
        jnp.dot(other_columns[col_order], inverse.T, precision=high),
        jnp.dot(columns[row_order], inverse.T, precision=high).T,
        precision=high,
    )
    live_rows = (global_rows >= PANEL) & (global_rows < own_order)
    live_cols = (global_cols >= PANEL) & (global_cols < own_order)
    turned = jnp.where(
        live_cols[col_order][:, None] & live_rows[row_order][None, :],
        turned_block - turned_panels,
        jnp.float32(0.0),
    )
    part_rows = rows_here // n_row
    part_cols = cols_here // (2 * n_col)
    pieces = (
        turned.reshape(2, n_col, part_cols, n_row, part_rows)
        .transpose(0, 3, 1, 2, 4)
        .reshape(-1, part_rows)
    )
    arrived = lax.all_to_all(
        pieces, ("child", "row", "col"), split_axis=0, concat_axis=0, tiled=True
    )
    arrived = (
        arrived.reshape(2, n_row, n_col, part_cols, part_rows)
        .transpose(0, 2, 3, 1, 4)
        .reshape(2, n_col * part_cols, rows_here)
    )
    col_owner = child_index * n_col + col_index
    assembled = parent_front
    for source in range(2):
        parent_map = index_maps[source]
        row_slots = select_rows(parent_map, row_index, parent_rows, rows_here)
        col_slots = select_rows(parent_map, col_owner, parent_cols, n_col * part_cols)
        row_lookup = invert_slots(row_slots, parent_rows)
        spread = jnp.einsum(
            "qi,pq->ip", arrived[source], one_hot(col_slots, parent_cols),
            precision=lax.Precision.HIGHEST,
        )
        padded = jnp.pad(spread, ((0, 1), (0, 0)))
        assembled = assembled + jnp.take(padded, row_lookup, axis=0)
    return (assembled, own_panel[None])


def solution(mesh):
    in_specs = (P("child", "row", "col"), P("row", ("child", "col")), P(), P())
    out_specs = (P("row", ("child", "col")), P("child", "row", None))
    return jax.shard_map(
        on_device, mesh=mesh, in_specs=in_specs, out_specs=out_specs, check_vma=False
    )
```

```python
import jax
import jax.numpy as jnp
from jax import lax
from jax.sharding import PartitionSpec as P

PANEL = 512
FRONT = 8192


def from_root(value, axis, source):
    kept = jnp.where(lax.axis_index(axis) == source, value, 0).astype(value.dtype)
    return lax.psum(kept, axis)


def spread_sum(value, axis):
    count = lax.axis_size(axis)
    pieces = value.reshape(count, value.shape[0] // count, value.shape[1])
    arrived = lax.all_to_all(pieces, axis, 0, 0, tiled=True)
    return lax.all_gather(arrived.sum(0), axis, axis=0, tiled=True)


def from_first(value, axis):
    count = lax.axis_size(axis)
    pieces = value.reshape(count, value.shape[0] // count, value.shape[1])
    arrived = lax.all_to_all(pieces, axis, 0, 0, tiled=True)
    return lax.all_gather(arrived[0], axis, axis=0, tiled=True)


def select_rows(parent_map, owner, width, count):
    everywhere = jnp.arange(FRONT, dtype=jnp.int32)
    keyed = jnp.where(parent_map // width == owner, everywhere, everywhere + FRONT)
    chosen = jnp.argsort(keyed)[:count]
    return parent_map[chosen] - owner * width


def invert_slots(slots, length):
    count = slots.shape[0]
    lookup = jnp.full((length,), count, jnp.int32)
    return lookup.at[slots].set(jnp.arange(count, dtype=jnp.int32))


def one_hot(order, size):
    positions = jnp.arange(size, dtype=jnp.int32)
    return (positions[:, None] == order[None, :]).astype(jnp.float32)


def exact_matmul(values, select):
    return jnp.dot(values, select, precision=lax.Precision.HIGHEST)


def factor_and_invert(matrix, size):
    count = matrix.shape[0] // size
    eye = jnp.eye(size, dtype=jnp.float32)
    high = lax.Precision.HIGHEST
    trailing = (matrix + matrix.T) * 0.5
    factor, inverse = {}, {}
    for k in range(count):
        factor[k, k] = jnp.linalg.cholesky(trailing[:size, :size])
        inverse[k, k] = lax.linalg.triangular_solve(
            factor[k, k], eye, left_side=True, lower=True
        )
        if k + 1 < count:
            panel = jnp.dot(trailing[size:, :size], inverse[k, k].T, precision=high)
            for i in range(k + 1, count):
                factor[i, k] = panel[(i - k - 1) * size:(i - k) * size]
            trailing = trailing[size:, size:] - jnp.dot(panel, panel.T, precision=high)
    for i in range(count):
        for j in range(i - 1, -1, -1):
            total = sum(
                jnp.dot(factor[i, k], inverse[k, j], precision=high) for k in range(j, i)
            )
            inverse[i, j] = -jnp.dot(inverse[i, i], total, precision=high)
    zero = jnp.zeros((size, size), jnp.float32)

    def assemble(blocks):
        return jnp.concatenate(
            [
                jnp.concatenate(
                    [blocks[i, j] if j <= i else zero for j in range(count)], axis=1
                )
                for i in range(count)
            ]
        )

    return assemble(factor), assemble(inverse)


def factor_panel(diag_factor, inverse, columns, global_rows, own_order):
    solved = jnp.dot(columns, inverse.T, precision=lax.Precision.HIGHEST)
    top_rows = jnp.pad(diag_factor, ((0, columns.shape[0] - PANEL), (0, 0)))
    result = jnp.where(global_rows[:, None] < PANEL, top_rows, solved)
    return jnp.where(global_rows[:, None] < own_order, result, jnp.float32(0.0))


def on_device(child_fronts, parent_front, index_maps, orders):
    block_here = child_fronts[0]
    rows_here, cols_here = block_here.shape
    child_index = lax.axis_index("child")
    row_index = lax.axis_index("row")
    col_index = lax.axis_index("col")
    n_row = lax.axis_size("row")
    n_col = lax.axis_size("col")
    own_map = lax.dynamic_index_in_dim(index_maps, child_index, 0, keepdims=False)
    own_order = lax.dynamic_index_in_dim(orders, child_index, 0, keepdims=False)
    global_rows = row_index * rows_here + jnp.arange(rows_here, dtype=jnp.int32)
    global_cols = col_index * cols_here + jnp.arange(cols_here, dtype=jnp.int32)
    columns = from_first(block_here[:, :PANEL], "col")
    parent_rows, parent_cols = parent_front.shape
    row_map = lax.dynamic_slice_in_dim(own_map, row_index * rows_here, rows_here)
    col_map = lax.dynamic_slice_in_dim(own_map, col_index * cols_here, cols_here)
    row_keys = row_map // parent_rows * rows_here + jnp.arange(rows_here, dtype=jnp.int32)
    col_keys = col_map // parent_cols * cols_here + jnp.arange(cols_here, dtype=jnp.int32)
    col_order = jnp.argsort(col_keys)
    row_order = jnp.argsort(row_keys)
    turned_block = jnp.einsum(
        "qj,iq->ji", one_hot(col_order, cols_here), block_here[row_order],
        precision=lax.Precision.HIGHEST,
    )
    sent = jnp.concatenate(
        [
            jnp.where(row_index == col_index, columns, 0),
            jnp.where(row_index == 0, columns[:PANEL], 0),
        ]
    )
    sent, row_order, col_order, turned_block = lax.optimization_barrier(
        (sent, row_order, col_order, turned_block)
    )
    received = spread_sum(sent, "row")
    other_columns, corner = received[:rows_here], received[rows_here:]
    diag_factor, inverse = factor_and_invert(corner, PANEL // 4)
    late_maps, diag_factor = lax.optimization_barrier((index_maps, diag_factor))
    own_panel = factor_panel(diag_factor, inverse, columns, global_rows, own_order)
    high = lax.Precision.HIGHEST
    turned_panels = jnp.dot(
        jnp.dot(other_columns[col_order], inverse.T, precision=high),
        jnp.dot(columns[row_order], inverse.T, precision=high).T,
        precision=high,
    )
    live_rows = (global_rows >= PANEL) & (global_rows < own_order)
    live_cols = (global_cols >= PANEL) & (global_cols < own_order)
    turned = jnp.where(
        live_cols[col_order][:, None] & live_rows[row_order][None, :],
        turned_block - turned_panels,
        jnp.float32(0.0),
    )
    part_rows = rows_here // n_row
    part_cols = cols_here // (2 * n_col)
    pieces = (
        turned.reshape(2, n_col, part_cols, n_row, part_rows)
        .transpose(0, 3, 1, 2, 4)
        .reshape(-1, part_rows)
    )
    arrived = lax.all_to_all(
        pieces, ("child", "row", "col"), split_axis=0, concat_axis=0, tiled=True
    )
    arrived = (
        arrived.reshape(2, n_row, n_col, part_cols, part_rows)
        .transpose(0, 2, 3, 1, 4)
        .reshape(2, n_col * part_cols, rows_here)
    )
    col_owner = child_index * n_col + col_index
    assembled = parent_front
    for source in range(2):
        parent_map = late_maps[source]
        row_slots = select_rows(parent_map, row_index, parent_rows, rows_here)
        col_slots = select_rows(parent_map, col_owner, parent_cols, n_col * part_cols)
        row_lookup = invert_slots(row_slots, parent_rows)
        spread = jnp.einsum(
            "qi,pq->ip", arrived[source], one_hot(col_slots, parent_cols),
            precision=lax.Precision.HIGHEST,
        )
        padded = jnp.pad(spread, ((0, 1), (0, 0)))
        assembled = assembled + jnp.take(padded, row_lookup, axis=0)
    return (assembled, own_panel[None])


def solution(mesh):
    in_specs = (P("child", "row", "col"), P("row", ("child", "col")), P(), P())
    out_specs = (P("row", ("child", "col")), P("child", "row", None))
    return jax.shard_map(
        on_device, mesh=mesh, in_specs=in_specs, out_specs=out_specs, check_vma=False
    )
```

```python
import jax
import jax.numpy as jnp
from jax import lax
from jax.sharding import PartitionSpec as P

PANEL = 512
FRONT = 8192


def from_root(value, axis, source):
    kept = jnp.where(lax.axis_index(axis) == source, value, 0).astype(value.dtype)
    return lax.psum(kept, axis)


def spread_sum(value, axis):
    count = lax.axis_size(axis)
    pieces = value.reshape(count, value.shape[0] // count, value.shape[1])
    arrived = lax.all_to_all(pieces, axis, 0, 0, tiled=True)
    return lax.all_gather(arrived.sum(0), axis, axis=0, tiled=True)


def from_first(value, axis):
    count = lax.axis_size(axis)
    pieces = value.reshape(count, value.shape[0] // count, value.shape[1])
    arrived = lax.all_to_all(pieces, axis, 0, 0, tiled=True)
    return lax.all_gather(arrived[0], axis, axis=0, tiled=True)


def select_rows(parent_map, owner, width, count):
    everywhere = jnp.arange(FRONT, dtype=jnp.int32)
    keyed = jnp.where(parent_map // width == owner, everywhere, everywhere + FRONT)
    chosen = jnp.argsort(keyed)[:count]
    return parent_map[chosen] - owner * width


def invert_slots(slots, length):
    count = slots.shape[0]
    lookup = jnp.full((length,), count, jnp.int32)
    return lookup.at[slots].set(jnp.arange(count, dtype=jnp.int32))


def one_hot(order, size):
    positions = jnp.arange(size, dtype=jnp.int32)
    return (positions[:, None] == order[None, :]).astype(jnp.float32)


def exact_matmul(values, select):
    return jnp.dot(values, select, precision=lax.Precision.HIGHEST)


def factor_and_invert(matrix, size):
    count = matrix.shape[0] // size
    eye = jnp.eye(size, dtype=jnp.float32)
    high = lax.Precision.HIGHEST
    trailing = (matrix + matrix.T) * 0.5
    factor, inverse = {}, {}
    for k in range(count):
        factor[k, k] = jnp.linalg.cholesky(trailing[:size, :size])
        inverse[k, k] = lax.linalg.triangular_solve(
            factor[k, k], eye, left_side=True, lower=True
        )
        if k + 1 < count:
            panel = jnp.dot(trailing[size:, :size], inverse[k, k].T, precision=high)
            for i in range(k + 1, count):
                factor[i, k] = panel[(i - k - 1) * size:(i - k) * size]
            trailing = trailing[size:, size:] - jnp.dot(panel, panel.T, precision=high)
    for i in range(count):
        for j in range(i - 1, -1, -1):
            total = sum(
                jnp.dot(factor[i, k], inverse[k, j], precision=high) for k in range(j, i)
            )
            inverse[i, j] = -jnp.dot(inverse[i, i], total, precision=high)
    zero = jnp.zeros((size, size), jnp.float32)

    def assemble(blocks):
        return jnp.concatenate(
            [
                jnp.concatenate(
                    [blocks[i, j] if j <= i else zero for j in range(count)], axis=1
                )
                for i in range(count)
            ]
        )

    return assemble(factor), assemble(inverse)


def factor_panel(diag_factor, inverse, columns, global_rows, own_order):
    solved = jnp.dot(columns, inverse.T, precision=lax.Precision.HIGHEST)
    top_rows = jnp.pad(diag_factor, ((0, columns.shape[0] - PANEL), (0, 0)))
    result = jnp.where(global_rows[:, None] < PANEL, top_rows, solved)
    return jnp.where(global_rows[:, None] < own_order, result, jnp.float32(0.0))


def on_device(child_fronts, parent_front, index_maps, orders):
    block_here = child_fronts[0]
    rows_here, cols_here = block_here.shape
    child_index = lax.axis_index("child")
    row_index = lax.axis_index("row")
    col_index = lax.axis_index("col")
    n_row = lax.axis_size("row")
    n_col = lax.axis_size("col")
    own_map = lax.dynamic_index_in_dim(index_maps, child_index, 0, keepdims=False)
    own_order = lax.dynamic_index_in_dim(orders, child_index, 0, keepdims=False)
    global_rows = row_index * rows_here + jnp.arange(rows_here, dtype=jnp.int32)
    global_cols = col_index * cols_here + jnp.arange(cols_here, dtype=jnp.int32)
    columns = from_first(block_here[:, :PANEL], "col")
    sent = jnp.concatenate(
        [
            jnp.where(row_index == col_index, columns, 0),
            jnp.where(row_index == 0, columns[:PANEL], 0),
        ]
    )
    received = spread_sum(sent, "row")
    other_columns, corner = received[:rows_here], received[rows_here:]
    diag_factor, inverse = factor_and_invert(corner, PANEL // 4)
    own_panel = factor_panel(diag_factor, inverse, columns, global_rows, own_order)
    other_panel = factor_panel(diag_factor, inverse, other_columns, global_cols, own_order)
    update = block_here - jnp.dot(own_panel, other_panel.T, precision=lax.Precision.HIGHEST)
    live_rows = (global_rows >= PANEL) & (global_rows < own_order)
    live_cols = (global_cols >= PANEL) & (global_cols < own_order)
    update = jnp.where(live_rows[:, None] & live_cols[None, :], update, jnp.float32(0.0))
    parent_rows, parent_cols = parent_front.shape
    row_map = lax.dynamic_slice_in_dim(own_map, row_index * rows_here, rows_here)
    col_map = lax.dynamic_slice_in_dim(own_map, col_index * cols_here, cols_here)
    row_keys = row_map // parent_rows * rows_here + jnp.arange(rows_here, dtype=jnp.int32)
    col_keys = col_map // parent_cols * cols_here + jnp.arange(cols_here, dtype=jnp.int32)
    col_order = jnp.argsort(col_keys)
    col_select = one_hot(col_order, cols_here)
    turned = jnp.einsum(
        "qj,iq->ji", col_select, update[jnp.argsort(row_keys)],
        precision=lax.Precision.HIGHEST,
    )
    part_rows = rows_here // n_row
    part_cols = cols_here // (2 * n_col)
    pieces = (
        turned.reshape(2, n_col, part_cols, n_row, part_rows)
        .transpose(0, 3, 1, 2, 4)
        .reshape(-1, part_rows)
    )
    arrived = lax.all_to_all(
        pieces, ("child", "row", "col"), split_axis=0, concat_axis=0, tiled=True
    )
    arrived = arrived.reshape(2, n_row, n_col * part_cols, part_rows)
    col_owner = child_index * n_col + col_index
    assembled = parent_front
    for source in range(2):
        parent_map = index_maps[source]
        row_slots = select_rows(parent_map, row_index, parent_rows, rows_here)
        col_slots = select_rows(parent_map, col_owner, parent_cols, n_col * part_cols)
        row_lookup = invert_slots(row_slots, parent_rows)
        spread = jnp.einsum(
            "rqa,pq->rap", arrived[source], one_hot(col_slots, parent_cols),
            precision=lax.Precision.HIGHEST,
        ).reshape(rows_here, parent_cols)
        padded = jnp.pad(spread, ((0, 1), (0, 0)))
        assembled = assembled + jnp.take(padded, row_lookup, axis=0)
    return (assembled, own_panel[None])


def solution(mesh):
    in_specs = (P("child", "row", "col"), P("row", ("child", "col")), P(), P())
    out_specs = (P("row", ("child", "col")), P("child", "row", None))
    return jax.shard_map(
        on_device, mesh=mesh, in_specs=in_specs, out_specs=out_specs, check_vma=False
    )
```

```python
import jax
import jax.numpy as jnp
from jax import lax
from jax.sharding import PartitionSpec as P

PANEL = 512
FRONT = 8192


def from_root(value, axis, source):
    kept = jnp.where(lax.axis_index(axis) == source, value, 0).astype(value.dtype)
    return lax.psum(kept, axis)


def spread_sum(value, axis):
    count = lax.axis_size(axis)
    pieces = value.reshape(count, value.shape[0] // count, value.shape[1])
    arrived = lax.all_to_all(pieces, axis, 0, 0, tiled=True)
    return lax.all_gather(arrived.sum(0), axis, axis=0, tiled=True)


def from_first(value, axis):
    count = lax.axis_size(axis)
    pieces = value.reshape(count, value.shape[0] // count, value.shape[1])
    arrived = lax.all_to_all(pieces, axis, 0, 0, tiled=True)
    return lax.all_gather(arrived[0], axis, axis=0, tiled=True)


def select_rows(parent_map, owner, width, count):
    everywhere = jnp.arange(FRONT, dtype=jnp.int32)
    keyed = jnp.where(parent_map // width == owner, everywhere, everywhere + FRONT)
    chosen = jnp.argsort(keyed)[:count]
    return parent_map[chosen] - owner * width


def invert_slots(slots, length):
    count = slots.shape[0]
    lookup = jnp.full((length,), count, jnp.int32)
    return lookup.at[slots].set(jnp.arange(count, dtype=jnp.int32))


def one_hot(order, size):
    positions = jnp.arange(size, dtype=jnp.int32)
    return (positions[:, None] == order[None, :]).astype(jnp.float32)


def exact_matmul(values, select):
    return jnp.dot(values, select, precision=lax.Precision.HIGHEST)


def factor_and_solve(matrix, columns, size):
    count = matrix.shape[0] // size
    eye = jnp.eye(size, dtype=jnp.float32)
    high = lax.Precision.HIGHEST
    trailing = (matrix + matrix.T) * 0.5
    factor, solved = {}, []
    for k in range(count):
        factor[k, k] = jnp.linalg.cholesky(trailing[:size, :size])
        inverse = lax.linalg.triangular_solve(factor[k, k], eye, left_side=True, lower=True)
        if k + 1 < count:
            panel = jnp.dot(trailing[size:, :size], inverse.T, precision=high)
            for i in range(k + 1, count):
                factor[i, k] = panel[(i - k - 1) * size:(i - k) * size]
            trailing = trailing[size:, size:] - jnp.dot(panel, panel.T, precision=high)
        block = columns[:, k * size:(k + 1) * size]
        if k:
            known = jnp.concatenate(solved, axis=1)
            coupling = jnp.concatenate([factor[k, j] for j in range(k)], axis=1)
            block = block - jnp.dot(known, coupling.T, precision=high)
        solved.append(jnp.dot(block, inverse.T, precision=high))
    zero = jnp.zeros((size, size), jnp.float32)
    lower = jnp.concatenate(
        [
            jnp.concatenate([factor[i, j] if j <= i else zero for j in range(count)], axis=1)
            for i in range(count)
        ]
    )
    return lower, jnp.concatenate(solved, axis=1)


def factor_panel(diag_factor, solved, global_rows, own_order):
    top_rows = jnp.pad(diag_factor, ((0, solved.shape[0] - PANEL), (0, 0)))
    result = jnp.where(global_rows[:, None] < PANEL, top_rows, solved)
    return jnp.where(global_rows[:, None] < own_order, result, jnp.float32(0.0))


def on_device(child_fronts, parent_front, index_maps, orders):
    block_here = child_fronts[0]
    rows_here, cols_here = block_here.shape
    child_index = lax.axis_index("child")
    row_index = lax.axis_index("row")
    col_index = lax.axis_index("col")
    n_row = lax.axis_size("row")
    n_col = lax.axis_size("col")
    own_map = lax.dynamic_index_in_dim(index_maps, child_index, 0, keepdims=False)
    own_order = lax.dynamic_index_in_dim(orders, child_index, 0, keepdims=False)
    global_rows = row_index * rows_here + jnp.arange(rows_here, dtype=jnp.int32)
    global_cols = col_index * cols_here + jnp.arange(cols_here, dtype=jnp.int32)
    columns = from_first(block_here[:, :PANEL], "col")
    sent = jnp.concatenate(
        [
            jnp.where(row_index == col_index, columns, 0),
            jnp.where(row_index == 0, columns[:PANEL], 0),
        ]
    )
    received = spread_sum(sent, "row")
    other_columns, corner = received[:rows_here], received[rows_here:]
    diag_factor, solved = factor_and_solve(
        corner, jnp.concatenate([columns, other_columns]), PANEL // 4
    )
    own_panel = factor_panel(diag_factor, solved[:rows_here], global_rows, own_order)
    other_panel = factor_panel(diag_factor, solved[rows_here:], global_cols, own_order)
    update = block_here - jnp.dot(own_panel, other_panel.T, precision=lax.Precision.HIGHEST)
    live_rows = (global_rows >= PANEL) & (global_rows < own_order)
    live_cols = (global_cols >= PANEL) & (global_cols < own_order)
    update = jnp.where(live_rows[:, None] & live_cols[None, :], update, jnp.float32(0.0))
    parent_rows, parent_cols = parent_front.shape
    row_map = lax.dynamic_slice_in_dim(own_map, row_index * rows_here, rows_here)
    col_map = lax.dynamic_slice_in_dim(own_map, col_index * cols_here, cols_here)
    row_keys = row_map // parent_rows * rows_here + jnp.arange(rows_here, dtype=jnp.int32)
    col_keys = col_map // parent_cols * cols_here + jnp.arange(cols_here, dtype=jnp.int32)
    col_order = jnp.argsort(col_keys)
    col_select = one_hot(col_order, cols_here)
    turned = jnp.einsum(
        "qj,iq->ji", col_select, update[jnp.argsort(row_keys)],
        precision=lax.Precision.HIGHEST,
    )
    part_rows = rows_here // n_row
    part_cols = cols_here // (2 * n_col)
    pieces = (
        turned.reshape(2, n_col, part_cols, n_row, part_rows)
        .transpose(0, 3, 1, 2, 4)
        .reshape(-1, part_rows)
    )
    arrived = lax.all_to_all(
        pieces, ("child", "row", "col"), split_axis=0, concat_axis=0, tiled=True
    )
    arrived = arrived.reshape(2, n_row, n_col * part_cols, part_rows)
    col_owner = child_index * n_col + col_index
    assembled = parent_front
    for source in range(2):
        parent_map = index_maps[source]
        row_slots = select_rows(parent_map, row_index, parent_rows, rows_here)
        col_slots = select_rows(parent_map, col_owner, parent_cols, n_col * part_cols)
        row_lookup = invert_slots(row_slots, parent_rows)
        spread = jnp.einsum(
            "rqa,pq->rap", arrived[source], one_hot(col_slots, parent_cols),
            precision=lax.Precision.HIGHEST,
        ).reshape(rows_here, parent_cols)
        padded = jnp.pad(spread, ((0, 1), (0, 0)))
        assembled = assembled + jnp.take(padded, row_lookup, axis=0)
    return (assembled, own_panel[None])


def solution(mesh):
    in_specs = (P("child", "row", "col"), P("row", ("child", "col")), P(), P())
    out_specs = (P("row", ("child", "col")), P("child", "row", None))
    return jax.shard_map(
        on_device, mesh=mesh, in_specs=in_specs, out_specs=out_specs, check_vma=False
    )
```

```python
import jax
import jax.numpy as jnp
from jax import lax
from jax.sharding import PartitionSpec as P

PANEL = 512
FRONT = 8192


def from_root(value, axis, source):
    kept = jnp.where(lax.axis_index(axis) == source, value, 0).astype(value.dtype)
    return lax.psum(kept, axis)


def spread_sum(value, axis):
    count = lax.axis_size(axis)
    pieces = value.reshape(count, value.shape[0] // count, value.shape[1])
    arrived = lax.all_to_all(pieces, axis, 0, 0, tiled=True)
    return lax.all_gather(arrived.sum(0), axis, axis=0, tiled=True)


def from_first(value, axis, gather=True):
    count = lax.axis_size(axis)
    pieces = value.reshape(count, value.shape[0] // count, value.shape[1])
    arrived = lax.all_to_all(pieces, axis, 0, 0, tiled=True)
    if not gather:
        return arrived[0]
    return lax.all_gather(arrived[0], axis, axis=0, tiled=True)


def select_rows(parent_map, owner, width, count):
    everywhere = jnp.arange(FRONT, dtype=jnp.int32)
    keyed = jnp.where(parent_map // width == owner, everywhere, everywhere + FRONT)
    chosen = jnp.argsort(keyed)[:count]
    return parent_map[chosen] - owner * width


def invert_slots(slots, length):
    count = slots.shape[0]
    lookup = jnp.full((length,), count, jnp.int32)
    return lookup.at[slots].set(jnp.arange(count, dtype=jnp.int32))


def one_hot(order, size):
    positions = jnp.arange(size, dtype=jnp.int32)
    return (positions[:, None] == order[None, :]).astype(jnp.float32)


def exact_matmul(values, select):
    return jnp.dot(values, select, precision=lax.Precision.HIGHEST)


def factor_and_invert(matrix, size):
    count = matrix.shape[0] // size
    eye = jnp.eye(size, dtype=jnp.float32)
    high = lax.Precision.HIGHEST
    trailing = (matrix + matrix.T) * 0.5
    factor, inverse = {}, {}
    for k in range(count):
        factor[k, k] = jnp.linalg.cholesky(trailing[:size, :size])
        inverse[k, k] = lax.linalg.triangular_solve(
            factor[k, k], eye, left_side=True, lower=True
        )
        if k + 1 < count:
            panel = jnp.dot(trailing[size:, :size], inverse[k, k].T, precision=high)
            for i in range(k + 1, count):
                factor[i, k] = panel[(i - k - 1) * size:(i - k) * size]
            trailing = trailing[size:, size:] - jnp.dot(panel, panel.T, precision=high)
    for i in range(count):
        for j in range(i - 1, -1, -1):
            total = sum(
                jnp.dot(factor[i, k], inverse[k, j], precision=high) for k in range(j, i)
            )
            inverse[i, j] = -jnp.dot(inverse[i, i], total, precision=high)
    zero = jnp.zeros((size, size), jnp.float32)

    def assemble(blocks):
        return jnp.concatenate(
            [
                jnp.concatenate(
                    [blocks[i, j] if j <= i else zero for j in range(count)], axis=1
                )
                for i in range(count)
            ]
        )

    return assemble(factor), assemble(inverse)


def factor_panel(diag_factor, inverse, columns, global_rows, own_order):
    solved = jnp.dot(columns, inverse.T, precision=lax.Precision.HIGHEST)
    top_rows = jnp.pad(diag_factor, ((0, columns.shape[0] - PANEL), (0, 0)))
    result = jnp.where(global_rows[:, None] < PANEL, top_rows, solved)
    return jnp.where(global_rows[:, None] < own_order, result, jnp.float32(0.0))


def on_device(child_fronts, parent_front, index_maps, orders):
    block_here = child_fronts[0]
    rows_here, cols_here = block_here.shape
    child_index = lax.axis_index("child")
    row_index = lax.axis_index("row")
    col_index = lax.axis_index("col")
    n_row = lax.axis_size("row")
    n_col = lax.axis_size("col")
    own_map = lax.dynamic_index_in_dim(index_maps, child_index, 0, keepdims=False)
    own_order = lax.dynamic_index_in_dim(orders, child_index, 0, keepdims=False)
    global_rows = row_index * rows_here + jnp.arange(rows_here, dtype=jnp.int32)
    global_cols = col_index * cols_here + jnp.arange(cols_here, dtype=jnp.int32)
    columns = from_first(block_here[:, :PANEL], "col")
    part_rows = rows_here // n_row
    own_piece = lax.dynamic_slice_in_dim(columns, col_index * part_rows, part_rows)
    pairs = [(n_col * a + b, n_col * b + a) for a in range(n_row) for b in range(n_col)]
    transposed_piece = lax.ppermute(own_piece, ("row", "col"), pairs)
    corner_piece = from_first(columns[:PANEL], "row", gather=False)
    gathered = lax.all_gather(
        jnp.concatenate([transposed_piece, corner_piece]), "row", axis=0, tiled=False
    )
    other_columns = gathered[:, :part_rows].reshape(rows_here, PANEL)
    corner = gathered[:, part_rows:].reshape(PANEL, PANEL)
    diag_factor, inverse = factor_and_invert(corner, PANEL // 4)
    own_panel = factor_panel(diag_factor, inverse, columns, global_rows, own_order)
    other_panel = factor_panel(diag_factor, inverse, other_columns, global_cols, own_order)
    update = block_here - jnp.dot(own_panel, other_panel.T, precision=lax.Precision.HIGHEST)
    live_rows = (global_rows >= PANEL) & (global_rows < own_order)
    live_cols = (global_cols >= PANEL) & (global_cols < own_order)
    update = jnp.where(live_rows[:, None] & live_cols[None, :], update, jnp.float32(0.0))
    parent_rows, parent_cols = parent_front.shape
    row_map = lax.dynamic_slice_in_dim(own_map, row_index * rows_here, rows_here)
    col_map = lax.dynamic_slice_in_dim(own_map, col_index * cols_here, cols_here)
    row_keys = row_map // parent_rows * rows_here + jnp.arange(rows_here, dtype=jnp.int32)
    col_keys = col_map // parent_cols * cols_here + jnp.arange(cols_here, dtype=jnp.int32)
    col_order = jnp.argsort(col_keys)
    col_select = one_hot(col_order, cols_here)
    turned = jnp.einsum(
        "qj,iq->ji", col_select, update[jnp.argsort(row_keys)],
        precision=lax.Precision.HIGHEST,
    )
    part_cols = cols_here // (2 * n_col)
    pieces = (
        turned.reshape(2, n_col, part_cols, n_row, part_rows)
        .transpose(0, 3, 1, 2, 4)
        .reshape(-1, part_rows)
    )
    arrived = lax.all_to_all(
        pieces, ("child", "row", "col"), split_axis=0, concat_axis=0, tiled=True
    )
    arrived = arrived.reshape(2, n_row, n_col * part_cols, part_rows)
    col_owner = child_index * n_col + col_index
    assembled = parent_front
    for source in range(2):
        parent_map = index_maps[source]
        row_slots = select_rows(parent_map, row_index, parent_rows, rows_here)
        col_slots = select_rows(parent_map, col_owner, parent_cols, n_col * part_cols)
        row_lookup = invert_slots(row_slots, parent_rows)
        spread = jnp.einsum(
            "rqa,pq->rap", arrived[source], one_hot(col_slots, parent_cols),
            precision=lax.Precision.HIGHEST,
        ).reshape(rows_here, parent_cols)
        padded = jnp.pad(spread, ((0, 1), (0, 0)))
        assembled = assembled + jnp.take(padded, row_lookup, axis=0)
    return (assembled, own_panel[None])


def solution(mesh):
    in_specs = (P("child", "row", "col"), P("row", ("child", "col")), P(), P())
    out_specs = (P("row", ("child", "col")), P("child", "row", None))
    return jax.shard_map(
        on_device, mesh=mesh, in_specs=in_specs, out_specs=out_specs, check_vma=False
    )
```

```python
import jax
import jax.numpy as jnp
from jax import lax
from jax.sharding import PartitionSpec as P

PANEL = 512
FRONT = 8192


def from_root(value, axis, source):
    kept = jnp.where(lax.axis_index(axis) == source, value, 0).astype(value.dtype)
    return lax.psum(kept, axis)


def spread_sum(value, axis):
    count = lax.axis_size(axis)
    pieces = value.reshape(count, value.shape[0] // count, value.shape[1])
    arrived = lax.all_to_all(pieces, axis, 0, 0, tiled=True)
    return lax.all_gather(arrived.sum(0), axis, axis=0, tiled=True)


def from_first(value, axis, gather=True):
    count = lax.axis_size(axis)
    pieces = value.reshape(count, value.shape[0] // count, value.shape[1])
    arrived = lax.all_to_all(pieces, axis, 0, 0, tiled=True)
    if not gather:
        return arrived[0]
    return lax.all_gather(arrived[0], axis, axis=0, tiled=True)


def select_rows(parent_map, owner, width, count):
    everywhere = jnp.arange(FRONT, dtype=jnp.int32)
    keyed = jnp.where(parent_map // width == owner, everywhere, everywhere + FRONT)
    chosen = jnp.argsort(keyed)[:count]
    return parent_map[chosen] - owner * width


def invert_slots(slots, length):
    count = slots.shape[0]
    lookup = jnp.full((length,), count, jnp.int32)
    return lookup.at[slots].set(jnp.arange(count, dtype=jnp.int32))


def one_hot(order, size):
    positions = jnp.arange(size, dtype=jnp.int32)
    return (positions[:, None] == order[None, :]).astype(jnp.float32)


def exact_matmul(values, select):
    return jnp.dot(values, select, precision=lax.Precision.HIGHEST)


def factor_and_invert(matrix, size):
    count = matrix.shape[0] // size
    eye = jnp.eye(size, dtype=jnp.float32)
    high = lax.Precision.HIGHEST
    trailing = (matrix + matrix.T) * 0.5
    factor, inverse = {}, {}
    for k in range(count):
        factor[k, k] = jnp.linalg.cholesky(trailing[:size, :size])
        inverse[k, k] = lax.linalg.triangular_solve(
            factor[k, k], eye, left_side=True, lower=True
        )
        if k + 1 < count:
            panel = jnp.dot(trailing[size:, :size], inverse[k, k].T, precision=high)
            for i in range(k + 1, count):
                factor[i, k] = panel[(i - k - 1) * size:(i - k) * size]
            trailing = trailing[size:, size:] - jnp.dot(panel, panel.T, precision=high)
    for i in range(count):
        for j in range(i - 1, -1, -1):
            total = sum(
                jnp.dot(factor[i, k], inverse[k, j], precision=high) for k in range(j, i)
            )
            inverse[i, j] = -jnp.dot(inverse[i, i], total, precision=high)
    zero = jnp.zeros((size, size), jnp.float32)

    def assemble(blocks):
        return jnp.concatenate(
            [
                jnp.concatenate(
                    [blocks[i, j] if j <= i else zero for j in range(count)], axis=1
                )
                for i in range(count)
            ]
        )

    return assemble(factor), assemble(inverse)


def factor_panel(diag_factor, inverse, columns, global_rows, own_order):
    solved = jnp.dot(columns, inverse.T, precision=lax.Precision.HIGHEST)
    top_rows = jnp.pad(diag_factor, ((0, columns.shape[0] - PANEL), (0, 0)))
    result = jnp.where(global_rows[:, None] < PANEL, top_rows, solved)
    return jnp.where(global_rows[:, None] < own_order, result, jnp.float32(0.0))


def on_device(child_fronts, parent_front, index_maps, orders):
    block_here = child_fronts[0]
    rows_here, cols_here = block_here.shape
    child_index = lax.axis_index("child")
    row_index = lax.axis_index("row")
    col_index = lax.axis_index("col")
    n_row = lax.axis_size("row")
    n_col = lax.axis_size("col")
    own_map = lax.dynamic_index_in_dim(index_maps, child_index, 0, keepdims=False)
    own_order = lax.dynamic_index_in_dim(orders, child_index, 0, keepdims=False)
    global_rows = row_index * rows_here + jnp.arange(rows_here, dtype=jnp.int32)
    global_cols = col_index * cols_here + jnp.arange(cols_here, dtype=jnp.int32)
    columns = from_first(block_here[:, :PANEL], "col")
    part_rows = rows_here // n_row
    own_piece = lax.dynamic_slice_in_dim(columns, col_index * part_rows, part_rows)
    pairs = [(n_col * a + b, n_col * b + a) for a in range(n_row) for b in range(n_col)]
    transposed_piece = lax.ppermute(own_piece, ("row", "col"), pairs)
    corner_rows = PANEL // n_row
    corner_piece = columns[:corner_rows]
    for target in range(1, n_row):
        moved = lax.ppermute(
            columns[target * corner_rows:(target + 1) * corner_rows], "row", [(0, target)]
        )
        corner_piece = jnp.where(row_index == target, moved, corner_piece)
    gathered = lax.all_gather(
        jnp.concatenate([transposed_piece, corner_piece]), "row", axis=0, tiled=False
    )
    other_columns = gathered[:, :part_rows].reshape(rows_here, PANEL)
    corner = gathered[:, part_rows:].reshape(PANEL, PANEL)
    diag_factor, inverse = factor_and_invert(corner, PANEL // 4)
    own_panel = factor_panel(diag_factor, inverse, columns, global_rows, own_order)
    other_panel = factor_panel(diag_factor, inverse, other_columns, global_cols, own_order)
    update = block_here - jnp.dot(own_panel, other_panel.T, precision=lax.Precision.HIGHEST)
    live_rows = (global_rows >= PANEL) & (global_rows < own_order)
    live_cols = (global_cols >= PANEL) & (global_cols < own_order)
    update = jnp.where(live_rows[:, None] & live_cols[None, :], update, jnp.float32(0.0))
    parent_rows, parent_cols = parent_front.shape
    row_map = lax.dynamic_slice_in_dim(own_map, row_index * rows_here, rows_here)
    col_map = lax.dynamic_slice_in_dim(own_map, col_index * cols_here, cols_here)
    row_keys = row_map // parent_rows * rows_here + jnp.arange(rows_here, dtype=jnp.int32)
    col_keys = col_map // parent_cols * cols_here + jnp.arange(cols_here, dtype=jnp.int32)
    col_order = jnp.argsort(col_keys)
    col_select = one_hot(col_order, cols_here)
    turned = jnp.einsum(
        "qj,iq->ji", col_select, update[jnp.argsort(row_keys)],
        precision=lax.Precision.HIGHEST,
    )
    part_cols = cols_here // (2 * n_col)
    pieces = (
        turned.reshape(2, n_col, part_cols, n_row, part_rows)
        .transpose(0, 3, 1, 2, 4)
        .reshape(-1, part_rows)
    )
    arrived = lax.all_to_all(
        pieces, ("child", "row", "col"), split_axis=0, concat_axis=0, tiled=True
    )
    arrived = arrived.reshape(2, n_row, n_col * part_cols, part_rows)
    col_owner = child_index * n_col + col_index
    assembled = parent_front
    for source in range(2):
        parent_map = index_maps[source]
        row_slots = select_rows(parent_map, row_index, parent_rows, rows_here)
        col_slots = select_rows(parent_map, col_owner, parent_cols, n_col * part_cols)
        row_lookup = invert_slots(row_slots, parent_rows)
        spread = jnp.einsum(
            "rqa,pq->rap", arrived[source], one_hot(col_slots, parent_cols),
            precision=lax.Precision.HIGHEST,
        ).reshape(rows_here, parent_cols)
        padded = jnp.pad(spread, ((0, 1), (0, 0)))
        assembled = assembled + jnp.take(padded, row_lookup, axis=0)
    return (assembled, own_panel[None])


def solution(mesh):
    in_specs = (P("child", "row", "col"), P("row", ("child", "col")), P(), P())
    out_specs = (P("row", ("child", "col")), P("child", "row", None))
    return jax.shard_map(
        on_device, mesh=mesh, in_specs=in_specs, out_specs=out_specs, check_vma=False
    )
```

```python
import jax
import jax.numpy as jnp
from jax import lax
from jax.sharding import PartitionSpec as P

PANEL = 512
FRONT = 8192


def from_root(value, axis, source):
    kept = jnp.where(lax.axis_index(axis) == source, value, 0).astype(value.dtype)
    return lax.psum(kept, axis)


def spread_sum(value, axis):
    count = lax.axis_size(axis)
    pieces = value.reshape(count, value.shape[0] // count, value.shape[1])
    arrived = lax.all_to_all(pieces, axis, 0, 0, tiled=True)
    return lax.all_gather(arrived.sum(0), axis, axis=0, tiled=True)


def from_first(value, axis, gather=True):
    count = lax.axis_size(axis)
    pieces = value.reshape(count, value.shape[0] // count, value.shape[1])
    arrived = lax.all_to_all(pieces, axis, 0, 0, tiled=True)
    if not gather:
        return arrived[0]
    return lax.all_gather(arrived[0], axis, axis=0, tiled=True)


def select_rows(parent_map, owner, width, count):
    everywhere = jnp.arange(FRONT, dtype=jnp.int32)
    keyed = jnp.where(parent_map // width == owner, everywhere, everywhere + FRONT)
    chosen = jnp.argsort(keyed)[:count]
    return parent_map[chosen] - owner * width


def invert_slots(slots, length):
    count = slots.shape[0]
    lookup = jnp.full((length,), count, jnp.int32)
    return lookup.at[slots].set(jnp.arange(count, dtype=jnp.int32))


def one_hot(order, size):
    positions = jnp.arange(size, dtype=jnp.int32)
    return (positions[:, None] == order[None, :]).astype(jnp.float32)


def exact_matmul(values, select):
    return jnp.dot(values, select, precision=lax.Precision.HIGHEST)


def factor_and_invert(matrix, size):
    count = matrix.shape[0] // size
    eye = jnp.eye(size, dtype=jnp.float32)
    high = lax.Precision.HIGHEST
    trailing = (matrix + matrix.T) * 0.5
    factor, inverse = {}, {}
    for k in range(count):
        factor[k, k] = jnp.linalg.cholesky(trailing[:size, :size])
        inverse[k, k] = lax.linalg.triangular_solve(
            factor[k, k], eye, left_side=True, lower=True
        )
        if k + 1 < count:
            panel = jnp.dot(trailing[size:, :size], inverse[k, k].T, precision=high)
            for i in range(k + 1, count):
                factor[i, k] = panel[(i - k - 1) * size:(i - k) * size]
            trailing = trailing[size:, size:] - jnp.dot(panel, panel.T, precision=high)
    for i in range(count):
        for j in range(i - 1, -1, -1):
            total = sum(
                jnp.dot(factor[i, k], inverse[k, j], precision=high) for k in range(j, i)
            )
            inverse[i, j] = -jnp.dot(inverse[i, i], total, precision=high)
    zero = jnp.zeros((size, size), jnp.float32)

    def assemble(blocks):
        return jnp.concatenate(
            [
                jnp.concatenate(
                    [blocks[i, j] if j <= i else zero for j in range(count)], axis=1
                )
                for i in range(count)
            ]
        )

    return assemble(factor), assemble(inverse)


def factor_panel(diag_factor, inverse, columns, global_rows, own_order):
    solved = jnp.dot(columns, inverse.T, precision=lax.Precision.HIGHEST)
    top_rows = jnp.pad(diag_factor, ((0, columns.shape[0] - PANEL), (0, 0)))
    result = jnp.where(global_rows[:, None] < PANEL, top_rows, solved)
    return jnp.where(global_rows[:, None] < own_order, result, jnp.float32(0.0))


def on_device(child_fronts, parent_front, index_maps, orders):
    block_here = child_fronts[0]
    rows_here, cols_here = block_here.shape
    child_index = lax.axis_index("child")
    row_index = lax.axis_index("row")
    col_index = lax.axis_index("col")
    n_row = lax.axis_size("row")
    n_col = lax.axis_size("col")
    own_map = lax.dynamic_index_in_dim(index_maps, child_index, 0, keepdims=False)
    own_order = lax.dynamic_index_in_dim(orders, child_index, 0, keepdims=False)
    global_rows = row_index * rows_here + jnp.arange(rows_here, dtype=jnp.int32)
    global_cols = col_index * cols_here + jnp.arange(cols_here, dtype=jnp.int32)
    panel_rows = rows_here // n_col
    first_piece = block_here[:panel_rows, :PANEL]
    for target in range(1, n_col):
        moved = lax.ppermute(
            block_here[target * panel_rows:(target + 1) * panel_rows, :PANEL], "col", [(0, target)]
        )
        first_piece = jnp.where(col_index == target, moved, first_piece)
    columns = lax.all_gather(first_piece, "col", axis=0, tiled=True)
    part_rows = rows_here // n_row
    own_piece = lax.dynamic_slice_in_dim(columns, col_index * part_rows, part_rows)
    pairs = [(n_col * a + b, n_col * b + a) for a in range(n_row) for b in range(n_col)]
    transposed_piece = lax.ppermute(own_piece, ("row", "col"), pairs)
    corner_rows = PANEL // n_row
    corner_piece = columns[:corner_rows]
    for target in range(1, n_row):
        moved = lax.ppermute(
            columns[target * corner_rows:(target + 1) * corner_rows], "row", [(0, target)]
        )
        corner_piece = jnp.where(row_index == target, moved, corner_piece)
    gathered = lax.all_gather(
        jnp.concatenate([transposed_piece, corner_piece]), "row", axis=0, tiled=False
    )
    other_columns = gathered[:, :part_rows].reshape(rows_here, PANEL)
    corner = gathered[:, part_rows:].reshape(PANEL, PANEL)
    diag_factor, inverse = factor_and_invert(corner, PANEL // 4)
    own_panel = factor_panel(diag_factor, inverse, columns, global_rows, own_order)
    other_panel = factor_panel(diag_factor, inverse, other_columns, global_cols, own_order)
    update = block_here - jnp.dot(own_panel, other_panel.T, precision=lax.Precision.HIGHEST)
    live_rows = (global_rows >= PANEL) & (global_rows < own_order)
    live_cols = (global_cols >= PANEL) & (global_cols < own_order)
    update = jnp.where(live_rows[:, None] & live_cols[None, :], update, jnp.float32(0.0))
    parent_rows, parent_cols = parent_front.shape
    row_map = lax.dynamic_slice_in_dim(own_map, row_index * rows_here, rows_here)
    col_map = lax.dynamic_slice_in_dim(own_map, col_index * cols_here, cols_here)
    row_keys = row_map // parent_rows * rows_here + jnp.arange(rows_here, dtype=jnp.int32)
    col_keys = col_map // parent_cols * cols_here + jnp.arange(cols_here, dtype=jnp.int32)
    col_order = jnp.argsort(col_keys)
    col_select = one_hot(col_order, cols_here)
    turned = jnp.einsum(
        "qj,iq->ji", col_select, update[jnp.argsort(row_keys)],
        precision=lax.Precision.HIGHEST,
    )
    part_cols = cols_here // (2 * n_col)
    pieces = (
        turned.reshape(2, n_col, part_cols, n_row, part_rows)
        .transpose(0, 3, 1, 2, 4)
        .reshape(-1, part_rows)
    )
    arrived = lax.all_to_all(
        pieces, ("child", "row", "col"), split_axis=0, concat_axis=0, tiled=True
    )
    arrived = arrived.reshape(2, n_row, n_col * part_cols, part_rows)
    col_owner = child_index * n_col + col_index
    assembled = parent_front
    for source in range(2):
        parent_map = index_maps[source]
        row_slots = select_rows(parent_map, row_index, parent_rows, rows_here)
        col_slots = select_rows(parent_map, col_owner, parent_cols, n_col * part_cols)
        row_lookup = invert_slots(row_slots, parent_rows)
        spread = jnp.einsum(
            "rqa,pq->rap", arrived[source], one_hot(col_slots, parent_cols),
            precision=lax.Precision.HIGHEST,
        ).reshape(rows_here, parent_cols)
        padded = jnp.pad(spread, ((0, 1), (0, 0)))
        assembled = assembled + jnp.take(padded, row_lookup, axis=0)
    return (assembled, own_panel[None])


def solution(mesh):
    in_specs = (P("child", "row", "col"), P("row", ("child", "col")), P(), P())
    out_specs = (P("row", ("child", "col")), P("child", "row", None))
    return jax.shard_map(
        on_device, mesh=mesh, in_specs=in_specs, out_specs=out_specs, check_vma=False
    )
```

```python
import jax
import jax.numpy as jnp
from jax import lax
from jax.sharding import PartitionSpec as P

PANEL = 512
FRONT = 8192


def from_root(value, axis, source):
    kept = jnp.where(lax.axis_index(axis) == source, value, 0).astype(value.dtype)
    return lax.psum(kept, axis)


def spread_sum(value, axis):
    count = lax.axis_size(axis)
    pieces = value.reshape(count, value.shape[0] // count, value.shape[1])
    arrived = lax.all_to_all(pieces, axis, 0, 0, tiled=True)
    return lax.all_gather(arrived.sum(0), axis, axis=0, tiled=True)


def from_first(value, axis, gather=True):
    count = lax.axis_size(axis)
    pieces = value.reshape(count, value.shape[0] // count, value.shape[1])
    arrived = lax.all_to_all(pieces, axis, 0, 0, tiled=True)
    if not gather:
        return arrived[0]
    return lax.all_gather(arrived[0], axis, axis=0, tiled=True)


def select_rows(parent_map, owner, width, count):
    everywhere = jnp.arange(FRONT, dtype=jnp.int32)
    keyed = jnp.where(parent_map // width == owner, everywhere, everywhere + FRONT)
    chosen = jnp.argsort(keyed)[:count]
    return parent_map[chosen] - owner * width


def invert_slots(slots, length):
    count = slots.shape[0]
    lookup = jnp.full((length,), count, jnp.int32)
    return lookup.at[slots].set(jnp.arange(count, dtype=jnp.int32))


def one_hot(order, size):
    positions = jnp.arange(size, dtype=jnp.int32)
    return (positions[:, None] == order[None, :]).astype(jnp.float32)


def exact_matmul(values, select):
    return jnp.dot(values, select, precision=lax.Precision.HIGHEST)


def factor_and_invert(matrix, size):
    count = matrix.shape[0] // size
    eye = jnp.eye(size, dtype=jnp.float32)
    high = lax.Precision.HIGHEST
    trailing = (matrix + matrix.T) * 0.5
    factor, inverse = {}, {}
    for k in range(count):
        factor[k, k] = jnp.linalg.cholesky(trailing[:size, :size])
        inverse[k, k] = lax.linalg.triangular_solve(
            factor[k, k], eye, left_side=True, lower=True
        )
        if k + 1 < count:
            panel = jnp.dot(trailing[size:, :size], inverse[k, k].T, precision=high)
            for i in range(k + 1, count):
                factor[i, k] = panel[(i - k - 1) * size:(i - k) * size]
            trailing = trailing[size:, size:] - jnp.dot(panel, panel.T, precision=high)
    for i in range(count):
        for j in range(i - 1, -1, -1):
            total = sum(
                jnp.dot(factor[i, k], inverse[k, j], precision=high) for k in range(j, i)
            )
            inverse[i, j] = -jnp.dot(inverse[i, i], total, precision=high)
    zero = jnp.zeros((size, size), jnp.float32)

    def assemble(blocks):
        return jnp.concatenate(
            [
                jnp.concatenate(
                    [blocks[i, j] if j <= i else zero for j in range(count)], axis=1
                )
                for i in range(count)
            ]
        )

    return assemble(factor), assemble(inverse)


def factor_panel(diag_factor, inverse, columns, global_rows, own_order):
    solved = jnp.dot(columns, inverse.T, precision=lax.Precision.HIGHEST)
    top_rows = jnp.pad(diag_factor, ((0, columns.shape[0] - PANEL), (0, 0)))
    result = jnp.where(global_rows[:, None] < PANEL, top_rows, solved)
    return jnp.where(global_rows[:, None] < own_order, result, jnp.float32(0.0))


def on_device(child_fronts, parent_front, index_maps, orders):
    block_here = child_fronts[0]
    rows_here, cols_here = block_here.shape
    child_index = lax.axis_index("child")
    row_index = lax.axis_index("row")
    col_index = lax.axis_index("col")
    n_row = lax.axis_size("row")
    n_col = lax.axis_size("col")
    own_map = lax.dynamic_index_in_dim(index_maps, child_index, 0, keepdims=False)
    own_order = lax.dynamic_index_in_dim(orders, child_index, 0, keepdims=False)
    global_rows = row_index * rows_here + jnp.arange(rows_here, dtype=jnp.int32)
    global_cols = col_index * cols_here + jnp.arange(cols_here, dtype=jnp.int32)
    panel_rows = rows_here // n_col
    first_piece = block_here[:panel_rows, :PANEL]
    for target in range(1, n_col):
        moved = lax.ppermute(
            block_here[target * panel_rows:(target + 1) * panel_rows, :PANEL], "col", [(0, target)]
        )
        first_piece = jnp.where(col_index == target, moved, first_piece)
    columns = lax.all_gather(first_piece, "col", axis=0, tiled=True)
    part_rows = rows_here // n_row
    own_piece = lax.dynamic_slice_in_dim(columns, col_index * part_rows, part_rows)
    pairs = [(n_col * a + b, n_col * b + a) for a in range(n_row) for b in range(n_col)]
    transposed_piece = lax.ppermute(own_piece, ("row", "col"), pairs)
    corner_rows = PANEL // n_row
    corner_piece = columns[:corner_rows]
    for target in range(1, n_row):
        moved = lax.ppermute(
            columns[target * corner_rows:(target + 1) * corner_rows], "row", [(0, target)]
        )
        corner_piece = jnp.where(row_index == target, moved, corner_piece)
    gathered = lax.all_gather(
        jnp.concatenate([transposed_piece, corner_piece]), "row", axis=0, tiled=False
    )
    other_columns = gathered[:, :part_rows].reshape(rows_here, PANEL)
    corner = gathered[:, part_rows:].reshape(PANEL, PANEL)
    diag_factor, inverse = factor_and_invert(corner, PANEL // 4)
    own_panel = factor_panel(diag_factor, inverse, columns, global_rows, own_order)
    other_panel = factor_panel(diag_factor, inverse, other_columns, global_cols, own_order)
    parent_rows, parent_cols = parent_front.shape
    row_map = lax.dynamic_slice_in_dim(own_map, row_index * rows_here, rows_here)
    col_map = lax.dynamic_slice_in_dim(own_map, col_index * cols_here, cols_here)
    row_keys = row_map // parent_rows * rows_here + jnp.arange(rows_here, dtype=jnp.int32)
    col_keys = col_map // parent_cols * cols_here + jnp.arange(cols_here, dtype=jnp.int32)
    col_order = jnp.argsort(col_keys)
    col_select = one_hot(col_order, cols_here)
    row_order = jnp.argsort(row_keys)
    live_rows = (global_rows >= PANEL) & (global_rows < own_order)
    live_cols = (global_cols >= PANEL) & (global_cols < own_order)
    update = block_here[row_order] - jnp.dot(
        own_panel[row_order], other_panel.T, precision=lax.Precision.HIGHEST
    )
    update = jnp.where(
        live_rows[row_order][:, None] & live_cols[None, :], update, jnp.float32(0.0)
    )
    turned = jnp.einsum(
        "qj,iq->ji", col_select, update, precision=lax.Precision.HIGHEST
    )
    part_cols = cols_here // (2 * n_col)
    pieces = (
        turned.reshape(2, n_col, part_cols, n_row, part_rows)
        .transpose(0, 3, 1, 2, 4)
        .reshape(-1, part_rows)
    )
    arrived = lax.all_to_all(
        pieces, ("child", "row", "col"), split_axis=0, concat_axis=0, tiled=True
    )
    arrived = arrived.reshape(2, n_row, n_col * part_cols, part_rows)
    col_owner = child_index * n_col + col_index
    assembled = parent_front
    for source in range(2):
        parent_map = index_maps[source]
        row_slots = select_rows(parent_map, row_index, parent_rows, rows_here)
        col_slots = select_rows(parent_map, col_owner, parent_cols, n_col * part_cols)
        row_lookup = invert_slots(row_slots, parent_rows)
        spread = jnp.einsum(
            "rqa,pq->rap", arrived[source], one_hot(col_slots, parent_cols),
            precision=lax.Precision.HIGHEST,
        ).reshape(rows_here, parent_cols)
        padded = jnp.pad(spread, ((0, 1), (0, 0)))
        assembled = assembled + jnp.take(padded, row_lookup, axis=0)
    return (assembled, own_panel[None])


def solution(mesh):
    in_specs = (P("child", "row", "col"), P("row", ("child", "col")), P(), P())
    out_specs = (P("row", ("child", "col")), P("child", "row", None))
    return jax.shard_map(
        on_device, mesh=mesh, in_specs=in_specs, out_specs=out_specs, check_vma=False
    )
```
